512 devices in a mesh: dp: 64 (over z, y), fsdp: 8 (over x, core).
Axes of the slice: x: 4, y: 4, z: 16, core: 2. Of those that a mesh axis runs over, the one named last changes fastest.
Arguments:
- tokens: bfloat16 [65536, 2048], P('dp', 'fsdp'), may hold values from -6 to 6
- norm_gain: bfloat16 [2048], replicated, may hold values from 0.25 to 1.75
- query_gain: bfloat16 [128], replicated, as said below
- key_gain: bfloat16 [128], replicated, as said below
- w_query: bfloat16 [2048, 2048], P('dp', 'fsdp'), as said below
- w_key: bfloat16 [2048, 1024], P('dp', 'fsdp'), as said below
- w_value: bfloat16 [2048, 1024], P('dp', 'fsdp'), may hold values from -0.125 to 0.125
- w_out: bfloat16 [2048, 2048], P('dp', 'fsdp'), may hold values from -0.125 to 0.125
- prompt_lengths: int32 [64, 8], replicated, may hold values from 1 to 512, 1024 in all within a row
- span_group: int32 [64, 64], replicated, may hold values from 0 to 63, as said below
Outputs:
- attention_update: bfloat16 [65536, 2048], P('dp', 'fsdp')
- kv_cache: bfloat16 [65536, 8, 256], P('dp', 'fsdp')
The draws below stay inside these ranges and needn't reach their ends.
Inputs may be any that keep to these rules, and one draw needn't show every extreme that they name: `prompt_lengths`: row g sums to 1024. `span_group`: row i names, in arrival order, the group of each of its 64 blocks of 16 rows; every group is named exactly 64 times in all; every row names exactly one group twice and leaves exactly one group out, and every group is the one named twice by exactly one row. `query_gain`: Positive. `key_gain`: Positive. `w_query`: entries of size about one over the square root of 2048. `w_key`: entries of size about one over the square root of 2048.
All inputs are finite; a program needn't handle non-finite values.
Results may differ from the reference program's by a relative error of at most 0.0075.
The reference program's roundings to bfloat16 on the way count: a program that leaves them out, or rounds other values in their place, can miss the bound.
Values may be sent and summed in bfloat16 or wider, within the bound.
No kernel may reach another device: no remote copies, remote signals or barrier semaphores. Data moves between devices by JAX's collectives and lax.ppermute only.
A program may use at most 64 MiB of HBM per device.

```python
import math
import jax
import jax.numpy as jnp
import numpy as np
from jax import lax

D = 2048
QH = 16
KVH = 8
HD = 128
GROUP_TOK = 1024
PROMPTS = 8
MAX_LEN = 512
ARRIVE = 16
TOKENS = 65536
N_DP = 64


def query_base(key):
    normal_part = jax.random.truncated_normal(jax.random.fold_in(key, 11), -4.0, 4.0, (D, QH * HD), jnp.float32)
    return normal_part / math.sqrt(D)


def draw_w_query(key, part):
    return query_base(key).astype(jnp.bfloat16)


def draw_w_key(key, part):
    own_part = jax.random.truncated_normal(jax.random.fold_in(key, 12), -4.0, 4.0, (D, KVH, HD), jnp.float32) / math.sqrt(D)
    mixed = own_part
    return mixed.reshape(D, KVH * HD).astype(jnp.bfloat16)


def draw_query_gain(key, part):
    gains = jax.random.uniform(jax.random.fold_in(key, 21), (HD,), jnp.float32, 0.7, 1.3)
    return gains.astype(jnp.bfloat16)


def draw_key_gain(key, part):
    gains = jax.random.uniform(jax.random.fold_in(key, 22), (HD,), jnp.float32, 0.7, 1.3)
    return gains.astype(jnp.bfloat16)


def draw_span_group(key, part):
    first_key = jax.random.fold_in(key, 31)
    second_key = jax.random.fold_in(key, 32)
    third_key = jax.random.fold_in(key, 33)
    sigma = jax.random.permutation(first_key, N_DP).astype(jnp.int32)
    offset = jax.random.randint(second_key, (), 1, N_DP).astype(jnp.int32)
    indices = jnp.arange(N_DP, dtype=jnp.int32)
    tau = sigma[(indices + offset) % N_DP]
    base_rows = jnp.where(indices[None, :] == tau[:, None], sigma[:, None], indices[None, :]).astype(jnp.int32)
    scores = jax.random.randint(third_key, (N_DP, N_DP), 0, 1048576).astype(jnp.int32) * N_DP + indices[None, :]
    shuffle = jnp.argsort(scores, axis=1, stable=True).astype(jnp.int32)
    return jnp.take_along_axis(base_rows, shuffle, axis=1).astype(jnp.int32)


def steps_of(stream_key, extent, split, low, largest):
    def one(dim, blocks):
        steps = jax.random.uniform(jax.random.fold_in(jax.random.fold_in(stream_key, 6), dim), (blocks,), jnp.float32, low / len(split), largest / len(split))
        return jnp.repeat(jnp.exp(steps), extent[dim] // blocks).reshape((-1,) + (1,) * (len(extent) - dim - 1))

    level = one(*split[0])
    for cut in split[1:]:
        level = level * one(*cut)
    return level


def split_up(amount, total, most, lean):
    loads = [(1 << 20) // math.isqrt(standing ** lean) + 1 for standing in range(2, amount + 1)]
    surplus, given = total - most - (amount - 1), [1] * (amount - 1)
    while surplus > 0:
        movable = [i for i in range(amount - 1) if given[i] < most]
        pool, budget = sum([loads[i] for i in movable]), surplus
        for i in movable:
            more = min(most - given[i], max(1, budget * loads[i] // pool), surplus)
            given[i] = given[i] + more
            surplus = surplus - more
    return np.array([most] + given)


def ragged_sizes(key, count, total, bound, lean):
    if count == 2:
        one = jax.random.randint(key, (), max(1, total - bound), min(bound, total - 1) + 1)
        return jnp.stack([one, total - one])
    sizes = jnp.asarray(split_up(count, total, bound, lean), jnp.int32)
    pairs = (count - 1) // 2
    source_of, taker = sizes[1:1 + 2 * pairs:2], sizes[2:2 + 2 * pairs:2]
    margin = jnp.minimum(source_of - 1, bound - taker)
    moved = jax.random.randint(jax.random.fold_in(key, 1), (pairs,), 0, 1 << 20) % (margin + 1)
    sizes = sizes.at[1:1 + 2 * pairs:2].set(source_of - moved).at[2:2 + 2 * pairs:2].set(taker + moved)
    return sizes[jax.random.permutation(jax.random.fold_in(key, 2), count)]


def normal_values(rng, dims, width, most, cuts=(), kind=jnp.bfloat16):
    factor_of = steps_of(rng, dims, cuts, -0.22, 0.18) if cuts else 1.0
    array = jax.random.normal(rng, dims, jnp.float32) * width * factor_of
    return jnp.minimum(jnp.maximum(array, -most), most).astype(kind)


def setup_inputs(seed: int = 0) -> dict:
    streams_of = jax.random.split(jax.random.key(seed), 11)
    return {
        "tokens": normal_values(streams_of[0], (TOKENS, D), 1.0, 6.0, ((0, 64), (1, 8))),
        "norm_gain": jnp.clip(1.0 + 0.15 * jax.random.normal(streams_of[1], (D,), jnp.float32), 0.25, 1.75).astype(jnp.bfloat16),
        "query_gain": draw_query_gain(jax.random.fold_in(streams_of[10], 71), 0),
        "key_gain": draw_key_gain(jax.random.fold_in(streams_of[10], 71), 0),
        "w_query": draw_w_query(jax.random.fold_in(streams_of[10], 71), 0),
        "w_key": draw_w_key(jax.random.fold_in(streams_of[10], 71), 0),
        "w_value": normal_values(streams_of[6], (D, KVH * HD), D ** -0.5, 0.125, ((0, 64), (1, 8))),
        "w_out": normal_values(streams_of[7], (QH * HD, D), (QH * HD) ** -0.5, 0.125, ((0, 64), (1, 8))),
        "prompt_lengths": jax.vmap(lambda own: ragged_sizes(own, PROMPTS, GROUP_TOK, MAX_LEN, 2))(jax.random.split(streams_of[8], N_DP)).reshape((N_DP, PROMPTS)).astype(jnp.int32),
        "span_group": draw_span_group(jax.random.fold_in(streams_of[10], 71), 0),
    }


epsilon = 1e-06
rope_base = 1000000.0

def head_norm(inputs, gains):
    floats = inputs.astype(jnp.float32)
    inv_rms = lax.rsqrt(lax.optimization_barrier(jnp.mean(floats * floats, axis=-1, keepdims=True)) + epsilon)
    return floats * inv_rms * gains.astype(jnp.float32)

def rotate(inputs, offsets):
    half_dim = inputs.shape[-1] // 2
    frequency = jnp.power(rope_base, -2.0 * jnp.arange(half_dim, dtype=jnp.float32) / inputs.shape[-1])
    angles = offsets.astype(jnp.float32)[:, None] * frequency[None, :]
    cosine = jnp.cos(angles)[:, None, :]
    sine_part = jnp.sin(angles)[:, None, :]
    first_half = inputs[..., :half_dim]
    second = inputs[..., half_dim:]
    return jnp.concatenate([first_half * cosine - second * sine_part, second * cosine + first_half * sine_part], axis=-1)

def prompt_layout(lengths, group_rows):
    prompt_end = jnp.cumsum(lengths).astype(jnp.int32)
    begins = (prompt_end - lengths).astype(jnp.int32)
    position = jnp.arange(group_rows, dtype=jnp.int32)
    inside = (position[:, None] >= begins[None, :]) & (position[:, None] < prompt_end[None, :])
    starts = lax.optimization_barrier(jnp.sum(jnp.where(inside, begins[None, :], 0), axis=1)).astype(jnp.int32)
    return (position, starts)

def reference(tokens, norm_gain, query_gain, key_gain, w_query, w_key, w_value, w_out, prompt_lengths, span_group):
    group_ids = jnp.arange(N_DP, dtype=jnp.int32)
    row_dest = jnp.repeat(span_group, ARRIVE, axis=1).astype(jnp.int32)
    onehot = (row_dest[:, :, None] == group_ids[None, None, :]).astype(jnp.int32)
    slot_rank = lax.optimization_barrier(jnp.sum((jnp.cumsum(onehot, axis=1) - 1) * onehot, axis=2)).astype(jnp.int32)
    counts = lax.optimization_barrier(jnp.sum((span_group[:, :, None] == group_ids[None, None, :]).astype(jnp.int32), axis=1)).astype(jnp.int32)
    offsets = (jnp.cumsum(counts, axis=0) - counts).astype(jnp.int32)
    own_offset = jnp.take_along_axis(offsets, row_dest, axis=1).astype(jnp.int32)
    group_position = (row_dest * GROUP_TOK + ARRIVE * own_offset + slot_rank).reshape(-1).astype(jnp.int32)
    order = jnp.zeros((TOKENS,), jnp.int32).at[group_position].set(jnp.arange(TOKENS, dtype=jnp.int32))
    grouped = tokens[order].reshape(N_DP, GROUP_TOK, D)
    group_ratio = QH // KVH
    scale = 1.0 / math.sqrt(HD)

    def one_group(pieces):
        rows_in, lengths = pieces
        position, starts = prompt_layout(lengths, GROUP_TOK)
        within = (position - starts).astype(jnp.int32)
        floats = rows_in.astype(jnp.float32)
        normed = (floats * lax.rsqrt(lax.optimization_barrier(jnp.mean(floats * floats, axis=-1, keepdims=True)) + epsilon) * norm_gain.astype(jnp.float32)).astype(jnp.bfloat16)
        query = jnp.dot(normed, w_query, preferred_element_type=jnp.float32).reshape(GROUP_TOK, QH, HD)
        key_rows = jnp.dot(normed, w_key, preferred_element_type=jnp.float32).reshape(GROUP_TOK, KVH, HD)
        value_rows = jnp.dot(normed, w_value, preferred_element_type=jnp.float32).reshape(GROUP_TOK, KVH, HD).astype(jnp.bfloat16)
        query_rot = rotate(head_norm(query, query_gain), within).astype(jnp.bfloat16)
        key_rot = rotate(head_norm(key_rows, key_gain), within).astype(jnp.bfloat16)
        query_heads = query_rot.reshape(GROUP_TOK, KVH, group_ratio, HD)
        scores = jnp.einsum('qkrd,skd->krqs', query_heads.astype(jnp.float32), key_rot.astype(jnp.float32)) * scale
        allowed = (position[None, :] <= position[:, None]) & (position[None, :] >= starts[:, None])
        masked = jnp.where(allowed[None, None], scores, -jnp.inf)
        row_max = lax.optimization_barrier(jnp.max(masked, axis=-1, keepdims=True))
        exp_scores = jnp.exp(masked - row_max)
        probs = (exp_scores / lax.optimization_barrier(jnp.sum(exp_scores, axis=-1, keepdims=True))).astype(jnp.bfloat16)
        heads_out = jnp.einsum('krqs,skd->qkrd', probs.astype(jnp.float32), value_rows.astype(jnp.float32)).astype(jnp.bfloat16)
        update = jnp.dot(heads_out.reshape(GROUP_TOK, QH * HD), w_out, preferred_element_type=jnp.float32).astype(jnp.bfloat16)
        cache_rows = jnp.concatenate([key_rot, value_rows], axis=-1)
        return (update, cache_rows)
    updates, caches = lax.map(one_group, (grouped, prompt_lengths))
    attention_update = updates.reshape(TOKENS, D)[group_position]
    kv_cache = caches.reshape(TOKENS, KVH, 2 * HD)[group_position]
    return (attention_update, kv_cache)
```

```python
import math

import jax
import jax.numpy as jnp
from jax import lax
from jax.sharding import Mesh, PartitionSpec as P

QH = 16
KVH = 8
HD = 128
DP = ("z", "y")


epsilon = 1e-06
rope_base = 1000000.0


def for_sending(x):

    def short(part):
        return part.astype(jnp.bfloat16) if part.dtype == jnp.float32 else part

    return jax.tree.map(short, x)


def head_norm(inputs, gains):
    inv_rms = lax.rsqrt(jnp.mean(inputs * inputs, axis=-1, keepdims=True) + epsilon)
    return inputs * inv_rms * gains.astype(jnp.float32)


def rotate(inputs, offsets):
    half_dim = inputs.shape[-1] // 2
    frequency = jnp.power(
        rope_base, -2.0 * jnp.arange(half_dim, dtype=jnp.float32) / inputs.shape[-1]
    )
    angles = offsets.astype(jnp.float32)[:, None] * frequency[None, :]
    cosine = jnp.cos(angles)[:, None, :]
    sine_part = jnp.sin(angles)[:, None, :]
    first_half = inputs[..., :half_dim]
    second = inputs[..., half_dim:]
    return jnp.concatenate(
        [first_half * cosine - second * sine_part, second * cosine + first_half * sine_part],
        axis=-1,
    )


def prompt_layout(lengths, group_rows):
    prompt_end = jnp.cumsum(lengths)
    begins = prompt_end - lengths
    position = jnp.arange(group_rows, dtype=jnp.int32)
    inside = (position[:, None] >= begins[None, :]) & (position[:, None] < prompt_end[None, :])
    starts = jnp.sum(jnp.where(inside, begins[None, :], 0), axis=1)
    return (position, starts)


def attend(query_block, key_rot, value_rows, pos_block, start_block, position):
    scores = jnp.einsum(
        "qkrd,skd->krqs", query_block, key_rot, preferred_element_type=jnp.float32
    ) * (1.0 / math.sqrt(HD))
    allowed = (position[None, :] <= pos_block[:, None]) & (
        position[None, :] >= start_block[:, None]
    )
    masked = jnp.where(allowed[None, None], scores, -jnp.inf)
    row_max = jnp.max(masked, axis=-1, keepdims=True)
    exp_scores = jnp.exp(masked - row_max)
    probs = (exp_scores / jnp.sum(exp_scores, axis=-1, keepdims=True)).astype(jnp.bfloat16)
    return jnp.einsum(
        "krqs,skd->qkrd", probs, value_rows, preferred_element_type=jnp.float32
    ).astype(jnp.bfloat16)


def with_zero_row(array):
    return jnp.concatenate([array, jnp.zeros((1,) + array.shape[1:], array.dtype)], axis=0)


def local(
    tokens,
    norm_gain,
    query_gain,
    key_gain,
    w_query,
    w_key,
    w_value,
    w_out,
    prompt_lengths,
    span_group,
):
    group_rows, width_local = tokens.shape
    groups = lax.axis_size(DP)
    arrival_rows = group_rows // groups
    capacity = 2 * arrival_rows
    device_index = lax.axis_index(DP)
    group_ids = jnp.arange(groups, dtype=jnp.int32)
    slot_ids = jnp.arange(capacity, dtype=jnp.int32)
    own_blocks = lax.dynamic_index_in_dim(span_group, device_index, 0, keepdims=False)
    counts = jnp.sum((span_group == device_index).astype(jnp.int32), axis=1)
    offsets = jnp.cumsum(counts) - counts
    row_dest = jnp.repeat(own_blocks, arrival_rows)
    onehot = (row_dest[:, None] == group_ids[None, :]).astype(jnp.int32)
    slot_rank = jnp.sum((jnp.cumsum(onehot, axis=0) - 1) * onehot, axis=1)
    send_slot = row_dest * capacity + slot_rank
    slot_source = (
        jnp.full((groups * capacity,), group_rows, jnp.int32)
        .at[send_slot]
        .set(jnp.arange(group_rows, dtype=jnp.int32))
    )
    outgoing = with_zero_row(tokens)[slot_source].reshape(groups, capacity, width_local)
    incoming = lax.all_to_all(outgoing, DP, split_axis=0, concat_axis=0, tiled=True)
    is_valid = slot_ids[None, :] < arrival_rows * counts[:, None]
    target = arrival_rows * offsets[:, None] + slot_ids[None, :]
    flat_slot = group_ids[:, None] * capacity + slot_ids[None, :]
    back_index = jnp.where(is_valid, target, group_rows)
    source_of = (
        jnp.zeros((group_rows,), jnp.int32)
        .at[back_index.reshape(-1)]
        .set(flat_slot.reshape(-1), mode="drop")
    )
    arrived = incoming.reshape(groups * capacity, width_local)[source_of]
    full_rows = lax.all_gather(arrived, "fsdp", axis=1, tiled=True)
    weights = jnp.concatenate([w_query, w_key, w_value, w_out], axis=1)
    weights = lax.all_gather(weights, "y", axis=0, tiled=True)
    weights = lax.all_gather(weights, "z", axis=0, tiled=True)
    cuts = [w_query.shape[1], w_key.shape[1], w_value.shape[1], w_out.shape[1]]
    bounds = [sum(cuts[:k]) for k in range(5)]
    query_full, key_full, value_full, out_full = (
        weights[:, bounds[k] : bounds[k + 1]] for k in range(4)
    )
    lengths = lax.dynamic_index_in_dim(prompt_lengths, device_index, 0, keepdims=False)
    position, starts = prompt_layout(lengths, group_rows)
    within = position - starts
    floats = full_rows.astype(jnp.float32)
    normed = (
        floats
        * lax.rsqrt(jnp.mean(floats * floats, axis=-1, keepdims=True) + epsilon)
        * norm_gain.astype(jnp.float32)
    ).astype(jnp.bfloat16)
    query = jnp.dot(normed, query_full, preferred_element_type=jnp.float32).reshape(
        group_rows, -1, HD
    )
    key_rows = jnp.dot(normed, key_full, preferred_element_type=jnp.float32).reshape(
        group_rows, -1, HD
    )
    value_rows = (
        jnp.dot(normed, value_full, preferred_element_type=jnp.float32)
        .reshape(group_rows, -1, HD)
        .astype(jnp.bfloat16)
    )
    query_rot = rotate(head_norm(query, query_gain), within).astype(jnp.bfloat16)
    key_rot = rotate(head_norm(key_rows, key_gain), within).astype(jnp.bfloat16)
    kv_heads = key_rot.shape[1]
    group_ratio = QH // KVH
    cache_rows = jnp.concatenate([key_rot, value_rows], axis=-1)
    block_count = group_rows // 512
    block_len = group_rows // block_count
    query_heads = query_rot.reshape(block_count, block_len, kv_heads, group_ratio, HD)

    def one_block(pieces):
        query_block, pos_block, start_block = pieces
        return attend(query_block, key_rot, value_rows, pos_block, start_block, position)

    mixed = lax.map(
        one_block,
        (
            query_heads,
            position.reshape(block_count, block_len),
            starts.reshape(block_count, block_len),
        ),
    )
    mixed = mixed.reshape(group_rows, kv_heads * group_ratio * HD)
    heads_all = lax.all_gather(mixed, "fsdp", axis=1, tiled=True)
    update = jnp.dot(heads_all, out_full, preferred_element_type=jnp.float32).astype(jnp.bfloat16)
    arrays = (update, cache_rows)
    sent = tuple((with_zero_row(array)[back_index] for array in arrays))
    back = jax.tree.map(
        lambda part, own: part.astype(own.dtype),
        lax.all_to_all(for_sending(sent), DP, split_axis=0, concat_axis=0, tiled=True),
        sent,
    )
    attention_out, cache_out = tuple(
        (piece.reshape((groups * capacity,) + piece.shape[2:])[send_slot] for piece in back)
    )
    return (attention_out, cache_out)


def solution(mesh):
    z_size = mesh.shape["dp"] // 4
    fine = Mesh(mesh.devices.reshape(z_size, 4, mesh.shape["fsdp"]), ("z", "y", "fsdp"))
    return jax.shard_map(
        local,
        mesh=fine,
        in_specs=(
            P(DP, "fsdp"),
            P(),
            P(),
            P(),
            P(DP, "fsdp"),
            P(DP, "fsdp"),
            P(DP, "fsdp"),
            P(DP, "fsdp"),
            P(),
            P(),
        ),
        out_specs=(P(DP, "fsdp"), P(DP, "fsdp", None)),
        check_vma=False,
    )
```

```python
import math

import jax
import jax.numpy as jnp
from jax import lax
from jax.sharding import Mesh, PartitionSpec as P

QH = 16
KVH = 8
HD = 128
DP = ("z", "y")


epsilon = 1e-06
rope_base = 1000000.0


def for_sending(x):

    def short(part):
        return part.astype(jnp.bfloat16) if part.dtype == jnp.float32 else part

    return jax.tree.map(short, x)


def head_norm(inputs, gains):
    inv_rms = lax.rsqrt(jnp.mean(inputs * inputs, axis=-1, keepdims=True) + epsilon)
    return inputs * inv_rms * gains.astype(jnp.float32)


def rotate(inputs, offsets):
    half_dim = inputs.shape[-1] // 2
    frequency = jnp.power(
        rope_base, -2.0 * jnp.arange(half_dim, dtype=jnp.float32) / inputs.shape[-1]
    )
    angles = offsets.astype(jnp.float32)[:, None] * frequency[None, :]
    cosine = jnp.cos(angles)[:, None, :]
    sine_part = jnp.sin(angles)[:, None, :]
    first_half = inputs[..., :half_dim]
    second = inputs[..., half_dim:]
    return jnp.concatenate(
        [first_half * cosine - second * sine_part, second * cosine + first_half * sine_part],
        axis=-1,
    )


def prompt_layout(lengths, group_rows):
    prompt_end = jnp.cumsum(lengths)
    begins = prompt_end - lengths
    position = jnp.arange(group_rows, dtype=jnp.int32)
    inside = (position[:, None] >= begins[None, :]) & (position[:, None] < prompt_end[None, :])
    starts = jnp.sum(jnp.where(inside, begins[None, :], 0), axis=1)
    return (position, starts)


def attend(query_block, key_rot, value_rows, pos_block, start_block, position):
    scores = jnp.einsum(
        "qkrd,skd->krqs", query_block, key_rot, preferred_element_type=jnp.float32
    ) * (1.0 / math.sqrt(HD))
    allowed = (position[None, :] <= pos_block[:, None]) & (
        position[None, :] >= start_block[:, None]
    )
    masked = jnp.where(allowed[None, None], scores, -jnp.inf)
    row_max = jnp.max(masked, axis=-1, keepdims=True)
    exp_scores = jnp.exp(masked - row_max)
    probs = (exp_scores / jnp.sum(exp_scores, axis=-1, keepdims=True)).astype(jnp.bfloat16)
    return jnp.einsum(
        "krqs,skd->qkrd", probs, value_rows, preferred_element_type=jnp.float32
    ).astype(jnp.bfloat16)


def local(
    tokens,
    norm_gain,
    query_gain,
    key_gain,
    w_query,
    w_key,
    w_value,
    w_out,
    prompt_lengths,
    span_group,
):
    group_rows, width_local = tokens.shape
    groups = lax.axis_size(DP)
    arrival_rows = group_rows // groups
    device_index = lax.axis_index(DP)
    block_ids = jnp.arange(groups, dtype=jnp.int32)

    weights = jnp.concatenate([w_query, w_key, w_value, w_out], axis=1)
    weights = lax.all_gather(weights, "y", axis=0, tiled=True)
    weights, tokens = lax.optimization_barrier((weights, tokens))
    weights = lax.all_gather(weights, "z", axis=0, tiled=True)

    own_blocks = lax.dynamic_index_in_dim(span_group, device_index, 0, keepdims=False)
    same = own_blocks[:, None] == own_blocks[None, :]
    dup_rank = jnp.sum(same & (block_ids[None, :] < block_ids[:, None]), axis=1).astype(jnp.int32)
    send_slot = own_blocks * 2 + dup_rank
    slot_source = jnp.zeros((groups * 2,), jnp.int32).at[send_slot].set(block_ids)
    token_blocks = tokens.reshape(groups, arrival_rows, width_local)
    outgoing = jnp.take(token_blocks, slot_source, axis=0, mode="clip").reshape(
        groups, 2 * arrival_rows, width_local
    )
    incoming = lax.all_to_all(outgoing, DP, split_axis=0, concat_axis=0, tiled=True)
    counts = jnp.sum((span_group == device_index).astype(jnp.int32), axis=1)
    offsets = jnp.cumsum(counts) - counts
    sub_ids = jnp.arange(2, dtype=jnp.int32)
    is_valid = sub_ids[None, :] < counts[:, None]
    back_index = jnp.where(is_valid, offsets[:, None] + sub_ids[None, :], groups)
    flat_slot = block_ids[:, None] * 2 + sub_ids[None, :]
    source_of = (
        jnp.zeros((groups,), jnp.int32)
        .at[back_index.reshape(-1)]
        .set(flat_slot.reshape(-1), mode="drop")
    )
    arrived = jnp.take(
        incoming.reshape(groups * 2, arrival_rows, width_local), source_of, axis=0, mode="clip"
    ).reshape(group_rows, width_local)
    arrived, weights = lax.optimization_barrier((arrived, weights))
    full_rows = lax.all_gather(arrived, "fsdp", axis=1, tiled=True)
    cuts = [w_query.shape[1], w_key.shape[1], w_value.shape[1], w_out.shape[1]]
    bounds = [sum(cuts[:k]) for k in range(5)]
    query_full, key_full, value_full, out_full = (
        weights[:, bounds[k] : bounds[k + 1]] for k in range(4)
    )
    lengths = lax.dynamic_index_in_dim(prompt_lengths, device_index, 0, keepdims=False)
    position, starts = prompt_layout(lengths, group_rows)
    within = position - starts
    floats = full_rows.astype(jnp.float32)
    normed = (
        floats
        * lax.rsqrt(jnp.mean(floats * floats, axis=-1, keepdims=True) + epsilon)
        * norm_gain.astype(jnp.float32)
    ).astype(jnp.bfloat16)
    query = jnp.dot(normed, query_full, preferred_element_type=jnp.float32).reshape(
        group_rows, -1, HD
    )
    key_rows = jnp.dot(normed, key_full, preferred_element_type=jnp.float32).reshape(
        group_rows, -1, HD
    )
    value_rows = (
        jnp.dot(normed, value_full, preferred_element_type=jnp.float32)
        .reshape(group_rows, -1, HD)
        .astype(jnp.bfloat16)
    )
    query_rot = rotate(head_norm(query, query_gain), within).astype(jnp.bfloat16)
    key_rot = rotate(head_norm(key_rows, key_gain), within).astype(jnp.bfloat16)
    kv_heads = key_rot.shape[1]
    group_ratio = QH // KVH
    cache_rows = jnp.concatenate([key_rot, value_rows], axis=-1)
    block_count = group_rows // 512
    block_len = group_rows // block_count
    query_heads = query_rot.reshape(block_count, block_len, kv_heads, group_ratio, HD)

    def one_block(pieces):
        query_block, pos_block, start_block = pieces
        return attend(query_block, key_rot, value_rows, pos_block, start_block, position)

    mixed = lax.map(
        one_block,
        (
            query_heads,
            position.reshape(block_count, block_len),
            starts.reshape(block_count, block_len),
        ),
    )
    mixed = mixed.reshape(group_rows, kv_heads * group_ratio * HD)
    heads_all = lax.all_gather(mixed, "fsdp", axis=1, tiled=True)
    update = jnp.dot(heads_all, out_full, preferred_element_type=jnp.float32).astype(jnp.bfloat16)
    cache_flat = cache_rows.reshape(group_rows, -1)
    update_width = update.shape[1]
    joined = jnp.concatenate([update, cache_flat], axis=1).reshape(groups, arrival_rows, -1)
    sent = jnp.take(joined, back_index.reshape(-1), axis=0, mode="clip").reshape(
        groups, 2 * arrival_rows, -1
    )
    back = lax.all_to_all(sent, DP, split_axis=0, concat_axis=0, tiled=True)
    mine = jnp.take(
        back.reshape(groups * 2, arrival_rows, -1), send_slot, axis=0, mode="clip"
    ).reshape(group_rows, -1)
    attention_out = mine[:, :update_width]
    cache_out = mine[:, update_width:].reshape(cache_rows.shape)
    return (attention_out, cache_out)


def solution(mesh):
    z_size = mesh.shape["dp"] // 4
    fine = Mesh(mesh.devices.reshape(z_size, 4, mesh.shape["fsdp"]), ("z", "y", "fsdp"))
    return jax.shard_map(
        local,
        mesh=fine,
        in_specs=(
            P(DP, "fsdp"),
            P(),
            P(),
            P(),
            P(DP, "fsdp"),
            P(DP, "fsdp"),
            P(DP, "fsdp"),
            P(DP, "fsdp"),
            P(),
            P(),
        ),
        out_specs=(P(DP, "fsdp"), P(DP, "fsdp", None)),
        check_vma=False,
    )
```

```python
import math

import jax
import jax.numpy as jnp
from jax import lax
from jax.sharding import Mesh, PartitionSpec as P

QH = 16
KVH = 8
HD = 128
DP = ("z", "y")


epsilon = 1e-06
rope_base = 1000000.0


def for_sending(x):

    def short(part):
        return part.astype(jnp.bfloat16) if part.dtype == jnp.float32 else part

    return jax.tree.map(short, x)


def head_norm(inputs, gains):
    inv_rms = lax.rsqrt(jnp.mean(inputs * inputs, axis=-1, keepdims=True) + epsilon)
    return inputs * inv_rms * gains.astype(jnp.float32)


def rotate(inputs, offsets):
    half_dim = inputs.shape[-1] // 2
    frequency = jnp.power(
        rope_base, -2.0 * jnp.arange(half_dim, dtype=jnp.float32) / inputs.shape[-1]
    )
    angles = offsets.astype(jnp.float32)[:, None] * frequency[None, :]
    cosine = jnp.cos(angles)[:, None, :]
    sine_part = jnp.sin(angles)[:, None, :]
    first_half = inputs[..., :half_dim]
    second = inputs[..., half_dim:]
    return jnp.concatenate(
        [first_half * cosine - second * sine_part, second * cosine + first_half * sine_part],
        axis=-1,
    )


def prompt_layout(lengths, group_rows):
    prompt_end = jnp.cumsum(lengths)
    begins = prompt_end - lengths
    position = jnp.arange(group_rows, dtype=jnp.int32)
    inside = (position[:, None] >= begins[None, :]) & (position[:, None] < prompt_end[None, :])
    starts = jnp.sum(jnp.where(inside, begins[None, :], 0), axis=1)
    return (position, starts)


def attend(query_block, key_rot, value_rows, pos_block, start_block, position):
    scores = jnp.einsum(
        "qkrd,skd->krqs", query_block, key_rot, preferred_element_type=jnp.float32
    ) * (1.0 / math.sqrt(HD))
    allowed = (position[None, :] <= pos_block[:, None]) & (
        position[None, :] >= start_block[:, None]
    )
    masked = jnp.where(allowed[None, None], scores, -jnp.inf)
    row_max = jnp.max(masked, axis=-1, keepdims=True)
    exp_scores = jnp.exp(masked - row_max)
    probs = (exp_scores / jnp.sum(exp_scores, axis=-1, keepdims=True)).astype(jnp.bfloat16)
    return jnp.einsum(
        "krqs,skd->qkrd", probs, value_rows, preferred_element_type=jnp.float32
    ).astype(jnp.bfloat16)


def local(
    tokens,
    norm_gain,
    query_gain,
    key_gain,
    w_query,
    w_key,
    w_value,
    w_out,
    prompt_lengths,
    span_group,
):
    group_rows, width_local = tokens.shape
    groups = lax.axis_size(DP)
    arrival_rows = group_rows // groups
    device_index = lax.axis_index(DP)
    block_ids = jnp.arange(groups, dtype=jnp.int32)

    own_blocks = lax.dynamic_index_in_dim(span_group, device_index, 0, keepdims=False)
    same = own_blocks[:, None] == own_blocks[None, :]
    dup_rank = jnp.sum(same & (block_ids[None, :] < block_ids[:, None]), axis=1).astype(jnp.int32)
    first_dest = jnp.where(dup_rank == 0, own_blocks, groups)
    slot_source = jnp.zeros((groups,), jnp.int32).at[first_dest].set(block_ids, mode="drop")
    dup_block = jnp.sum(jnp.where(dup_rank == 1, block_ids, 0))
    token_blocks = tokens.reshape(groups, arrival_rows, width_local)
    dup_tokens = lax.dynamic_index_in_dim(token_blocks, dup_block, 0, keepdims=False)

    weights = jnp.concatenate([w_query, w_key, w_value, w_out], axis=1)
    weight_rows, weight_width = weights.shape
    dup_size = arrival_rows * width_local
    dup_rows = -(-dup_size // weight_width)
    dup_flat = jnp.pad(dup_tokens.reshape(-1), (0, dup_rows * weight_width - dup_size))
    packed = jnp.concatenate([weights, dup_flat.reshape(dup_rows, weight_width)], axis=0)
    packed = lax.all_gather(packed, "y", axis=0, tiled=True)
    packed, token_blocks = lax.optimization_barrier((packed, token_blocks))
    packed = lax.all_gather(packed, "z", axis=0, tiled=True)
    packed = packed.reshape(groups, weight_rows + dup_rows, weight_width)
    weights = packed[:, :weight_rows].reshape(groups * weight_rows, weight_width)
    dup_all = (
        packed[:, weight_rows:]
        .reshape(groups, -1)[:, :dup_size]
        .reshape(groups, arrival_rows, width_local)
    )

    outgoing = jnp.take(token_blocks, slot_source, axis=0, mode="clip")
    incoming = lax.all_to_all(outgoing, DP, split_axis=0, concat_axis=0, tiled=True)
    counts = jnp.sum((span_group == device_index).astype(jnp.int32), axis=1)
    offsets = jnp.cumsum(counts) - counts
    first_pos = jnp.where(counts >= 1, offsets, groups)
    second_pos = jnp.where(counts == 2, offsets + 1, groups)
    source_of = (
        jnp.zeros((groups,), jnp.int32)
        .at[first_pos]
        .set(block_ids, mode="drop")
        .at[second_pos]
        .set(block_ids + groups, mode="drop")
    )
    pool = jnp.concatenate([incoming, dup_all], axis=0)
    arrived = jnp.take(pool, source_of, axis=0, mode="clip").reshape(group_rows, width_local)
    arrived, weights = lax.optimization_barrier((arrived, weights))
    full_rows = lax.all_gather(arrived, "fsdp", axis=1, tiled=True)
    cuts = [w_query.shape[1], w_key.shape[1], w_value.shape[1], w_out.shape[1]]
    bounds = [sum(cuts[:k]) for k in range(5)]
    query_full, key_full, value_full, out_full = (
        weights[:, bounds[k] : bounds[k + 1]] for k in range(4)
    )
    lengths = lax.dynamic_index_in_dim(prompt_lengths, device_index, 0, keepdims=False)
    position, starts = prompt_layout(lengths, group_rows)
    within = position - starts
    floats = full_rows.astype(jnp.float32)
    normed = (
        floats
        * lax.rsqrt(jnp.mean(floats * floats, axis=-1, keepdims=True) + epsilon)
        * norm_gain.astype(jnp.float32)
    ).astype(jnp.bfloat16)
    query = jnp.dot(normed, query_full, preferred_element_type=jnp.float32).reshape(
        group_rows, -1, HD
    )
    key_rows = jnp.dot(normed, key_full, preferred_element_type=jnp.float32).reshape(
        group_rows, -1, HD
    )
    value_rows = (
        jnp.dot(normed, value_full, preferred_element_type=jnp.float32)
        .reshape(group_rows, -1, HD)
        .astype(jnp.bfloat16)
    )
    query_rot = rotate(head_norm(query, query_gain), within).astype(jnp.bfloat16)
    key_rot = rotate(head_norm(key_rows, key_gain), within).astype(jnp.bfloat16)
    kv_heads = key_rot.shape[1]
    group_ratio = QH // KVH
    cache_rows = jnp.concatenate([key_rot, value_rows], axis=-1)
    block_count = group_rows // 512
    block_len = group_rows // block_count
    query_heads = query_rot.reshape(block_count, block_len, kv_heads, group_ratio, HD)

    def one_block(pieces):
        query_block, pos_block, start_block = pieces
        return attend(query_block, key_rot, value_rows, pos_block, start_block, position)

    mixed = lax.map(
        one_block,
        (
            query_heads,
            position.reshape(block_count, block_len),
            starts.reshape(block_count, block_len),
        ),
    )
    mixed = mixed.reshape(group_rows, kv_heads * group_ratio * HD)
    heads_all = lax.all_gather(mixed, "fsdp", axis=1, tiled=True)
    update = jnp.dot(heads_all, out_full, preferred_element_type=jnp.float32).astype(jnp.bfloat16)
    cache_flat = cache_rows.reshape(group_rows, -1)
    update_width = update.shape[1]
    joined = jnp.concatenate([update, cache_flat], axis=1).reshape(groups, arrival_rows, -1)
    sent = jnp.take(joined, offsets, axis=0, mode="clip")
    dup_position = jnp.sum(jnp.where(counts == 2, offsets + 1, 0))
    dup_result = lax.dynamic_index_in_dim(joined, dup_position, 0, keepdims=True)
    dup_result = lax.all_gather(dup_result, "y", axis=0, tiled=True)
    dup_result = lax.all_gather(dup_result, "z", axis=0, tiled=True)
    back = lax.all_to_all(sent, DP, split_axis=0, concat_axis=0, tiled=True)
    pool_back = jnp.concatenate([back, dup_result], axis=0)
    mine = jnp.take(
        pool_back, own_blocks + groups * dup_rank, axis=0, mode="clip"
    ).reshape(group_rows, -1)
    attention_out = mine[:, :update_width]
    cache_out = mine[:, update_width:].reshape(cache_rows.shape)
    return (attention_out, cache_out)


def solution(mesh):
    z_size = mesh.shape["dp"] // 4
    fine = Mesh(mesh.devices.reshape(z_size, 4, mesh.shape["fsdp"]), ("z", "y", "fsdp"))
    return jax.shard_map(
        local,
        mesh=fine,
        in_specs=(
            P(DP, "fsdp"),
            P(),
            P(),
            P(),
            P(DP, "fsdp"),
            P(DP, "fsdp"),
            P(DP, "fsdp"),
            P(DP, "fsdp"),
            P(),
            P(),
        ),
        out_specs=(P(DP, "fsdp"), P(DP, "fsdp", None)),
        check_vma=False,
    )
```

```python
import math

import jax
import jax.numpy as jnp
from jax import lax
from jax.sharding import Mesh, PartitionSpec as P

QH = 16
KVH = 8
HD = 128
DP = ("z_hi", "z_lo", "y")


epsilon = 1e-06
rope_base = 1000000.0


def for_sending(x):

    def short(part):
        return part.astype(jnp.bfloat16) if part.dtype == jnp.float32 else part

    return jax.tree.map(short, x)


def head_norm(inputs, gains):
    inv_rms = lax.rsqrt(jnp.mean(inputs * inputs, axis=-1, keepdims=True) + epsilon)
    return inputs * inv_rms * gains.astype(jnp.float32)


def rotate(inputs, offsets):
    half_dim = inputs.shape[-1] // 2
    frequency = jnp.power(
        rope_base, -2.0 * jnp.arange(half_dim, dtype=jnp.float32) / inputs.shape[-1]
    )
    angles = offsets.astype(jnp.float32)[:, None] * frequency[None, :]
    cosine = jnp.cos(angles)[:, None, :]
    sine_part = jnp.sin(angles)[:, None, :]
    first_half = inputs[..., :half_dim]
    second = inputs[..., half_dim:]
    return jnp.concatenate(
        [first_half * cosine - second * sine_part, second * cosine + first_half * sine_part],
        axis=-1,
    )


def prompt_layout(lengths, group_rows):
    prompt_end = jnp.cumsum(lengths)
    begins = prompt_end - lengths
    position = jnp.arange(group_rows, dtype=jnp.int32)
    inside = (position[:, None] >= begins[None, :]) & (position[:, None] < prompt_end[None, :])
    starts = jnp.sum(jnp.where(inside, begins[None, :], 0), axis=1)
    return (position, starts)


def attend(query_block, key_rot, value_rows, pos_block, start_block, position):
    scores = jnp.einsum(
        "qkrd,skd->krqs", query_block, key_rot, preferred_element_type=jnp.float32
    ) * (1.0 / math.sqrt(HD))
    allowed = (position[None, :] <= pos_block[:, None]) & (
        position[None, :] >= start_block[:, None]
    )
    masked = jnp.where(allowed[None, None], scores, -jnp.inf)
    row_max = jnp.max(masked, axis=-1, keepdims=True)
    exp_scores = jnp.exp(masked - row_max)
    probs = (exp_scores / jnp.sum(exp_scores, axis=-1, keepdims=True)).astype(jnp.bfloat16)
    return jnp.einsum(
        "krqs,skd->qkrd", probs, value_rows, preferred_element_type=jnp.float32
    ).astype(jnp.bfloat16)


def local(
    tokens,
    norm_gain,
    query_gain,
    key_gain,
    w_query,
    w_key,
    w_value,
    w_out,
    prompt_lengths,
    span_group,
):
    group_rows, width_local = tokens.shape
    groups = lax.axis_size(DP)
    arrival_rows = group_rows // groups
    device_index = lax.axis_index(DP)
    block_ids = jnp.arange(groups, dtype=jnp.int32)

    own_blocks = lax.dynamic_index_in_dim(span_group, device_index, 0, keepdims=False)
    same = own_blocks[:, None] == own_blocks[None, :]
    dup_rank = jnp.sum(same & (block_ids[None, :] < block_ids[:, None]), axis=1).astype(jnp.int32)
    first_dest = jnp.where(dup_rank == 0, own_blocks, groups)
    slot_source = jnp.zeros((groups,), jnp.int32).at[first_dest].set(block_ids, mode="drop")
    dup_block = jnp.sum(jnp.where(dup_rank == 1, block_ids, 0))
    token_blocks = tokens.reshape(groups, arrival_rows, width_local)
    dup_tokens = lax.dynamic_index_in_dim(token_blocks, dup_block, 0, keepdims=False)

    weights = jnp.concatenate([w_query, w_key, w_value, w_out], axis=1)
    weight_rows, weight_width = weights.shape
    packed = jnp.concatenate([weights, dup_tokens.reshape(weight_rows, -1)], axis=1)
    packed = lax.all_gather(packed, "y", axis=0, tiled=True)
    packed, token_blocks = lax.optimization_barrier((packed, token_blocks))
    packed = lax.all_gather(packed, "z_lo", axis=0, tiled=True)
    packed = lax.all_gather(packed, "z_hi", axis=0, tiled=True)
    weights = packed[:, :weight_width]
    dup_all = packed[:, weight_width:].reshape(groups, arrival_rows, width_local)

    outgoing = jnp.take(token_blocks, slot_source, axis=0, mode="clip")
    incoming = lax.all_to_all(outgoing, DP, split_axis=0, concat_axis=0, tiled=True)
    counts = jnp.sum((span_group == device_index).astype(jnp.int32), axis=1)
    offsets = jnp.cumsum(counts) - counts
    first_pos = jnp.where(counts >= 1, offsets, groups)
    second_pos = jnp.where(counts == 2, offsets + 1, groups)
    source_of = (
        jnp.zeros((groups,), jnp.int32)
        .at[first_pos]
        .set(block_ids, mode="drop")
        .at[second_pos]
        .set(block_ids + groups, mode="drop")
    )
    pool = jnp.concatenate([incoming, dup_all], axis=0)
    arrived = jnp.take(pool, source_of, axis=0, mode="clip").reshape(group_rows, width_local)
    arrived, weights = lax.optimization_barrier((arrived, weights))
    full_rows = lax.all_gather(arrived, "fsdp", axis=1, tiled=True)
    cuts = [w_query.shape[1], w_key.shape[1], w_value.shape[1], w_out.shape[1]]
    bounds = [sum(cuts[:k]) for k in range(5)]
    query_full, key_full, value_full, out_full = (
        weights[:, bounds[k] : bounds[k + 1]] for k in range(4)
    )
    lengths = lax.dynamic_index_in_dim(prompt_lengths, device_index, 0, keepdims=False)
    position, starts = prompt_layout(lengths, group_rows)
    within = position - starts
    floats = full_rows.astype(jnp.float32)
    normed = (
        floats
        * lax.rsqrt(jnp.mean(floats * floats, axis=-1, keepdims=True) + epsilon)
        * norm_gain.astype(jnp.float32)
    ).astype(jnp.bfloat16)
    query = jnp.dot(normed, query_full, preferred_element_type=jnp.float32).reshape(
        group_rows, -1, HD
    )
    key_rows = jnp.dot(normed, key_full, preferred_element_type=jnp.float32).reshape(
        group_rows, -1, HD
    )
    value_rows = (
        jnp.dot(normed, value_full, preferred_element_type=jnp.float32)
        .reshape(group_rows, -1, HD)
        .astype(jnp.bfloat16)
    )
    query_rot = rotate(head_norm(query, query_gain), within).astype(jnp.bfloat16)
    key_rot = rotate(head_norm(key_rows, key_gain), within).astype(jnp.bfloat16)
    kv_heads = key_rot.shape[1]
    group_ratio = QH // KVH
    cache_rows = jnp.concatenate([key_rot, value_rows], axis=-1)
    block_count = group_rows // 512
    block_len = group_rows // block_count
    query_heads = query_rot.reshape(block_count, block_len, kv_heads, group_ratio, HD)

    def one_block(pieces):
        query_block, pos_block, start_block = pieces
        return attend(query_block, key_rot, value_rows, pos_block, start_block, position)

    mixed = lax.map(
        one_block,
        (
            query_heads,
            position.reshape(block_count, block_len),
            starts.reshape(block_count, block_len),
        ),
    )
    mixed = mixed.reshape(group_rows, kv_heads * group_ratio * HD)
    heads_all = lax.all_gather(mixed, "fsdp", axis=1, tiled=True)
    update = jnp.dot(heads_all, out_full, preferred_element_type=jnp.float32).astype(jnp.bfloat16)
    cache_flat = cache_rows.reshape(group_rows, -1)
    update_width = update.shape[1]
    joined = jnp.concatenate([update, cache_flat], axis=1).reshape(groups, arrival_rows, -1)
    sent = jnp.take(joined, offsets, axis=0, mode="clip")
    dup_position = jnp.sum(jnp.where(counts == 2, offsets + 1, 0))
    dup_result = lax.dynamic_index_in_dim(joined, dup_position, 0, keepdims=True)
    dup_result = lax.all_gather(dup_result, "y", axis=0, tiled=True)
    dup_result = lax.all_gather(dup_result, "z_lo", axis=0, tiled=True)
    dup_result = lax.all_gather(dup_result, "z_hi", axis=0, tiled=True)
    back = lax.all_to_all(sent, DP, split_axis=0, concat_axis=0, tiled=True)
    pool_back = jnp.concatenate([back, dup_result], axis=0)
    mine = jnp.take(
        pool_back, own_blocks + groups * dup_rank, axis=0, mode="clip"
    ).reshape(group_rows, -1)
    attention_out = mine[:, :update_width]
    cache_out = mine[:, update_width:].reshape(cache_rows.shape)
    return (attention_out, cache_out)


def solution(mesh):
    z_size = mesh.shape["dp"] // 4
    fine = Mesh(
        mesh.devices.reshape(z_size // 4, 4, 4, mesh.shape["fsdp"]), ("z_hi", "z_lo", "y", "fsdp")
    )
    return jax.shard_map(
        local,
        mesh=fine,
        in_specs=(
            P(DP, "fsdp"),
            P(),
            P(),
            P(),
            P(DP, "fsdp"),
            P(DP, "fsdp"),
            P(DP, "fsdp"),
            P(DP, "fsdp"),
            P(),
            P(),
        ),
        out_specs=(P(DP, "fsdp"), P(DP, "fsdp", None)),
        check_vma=False,
    )
```

```python
import math

import jax
import jax.numpy as jnp
from jax import lax
from jax.sharding import Mesh, PartitionSpec as P

QH = 16
KVH = 8
HD = 128
DP = ("z", "y")


epsilon = 1e-06
rope_base = 1000000.0


def for_sending(x):

    def short(part):
        return part.astype(jnp.bfloat16) if part.dtype == jnp.float32 else part

    return jax.tree.map(short, x)


def head_norm(inputs, gains):
    inv_rms = lax.rsqrt(jnp.mean(inputs * inputs, axis=-1, keepdims=True) + epsilon)
    return inputs * inv_rms * gains.astype(jnp.float32)


def rotate(inputs, offsets):
    half_dim = inputs.shape[-1] // 2
    frequency = jnp.power(
        rope_base, -2.0 * jnp.arange(half_dim, dtype=jnp.float32) / inputs.shape[-1]
    )
    angles = offsets.astype(jnp.float32)[:, None] * frequency[None, :]
    cosine = jnp.cos(angles)[:, None, :]
    sine_part = jnp.sin(angles)[:, None, :]
    first_half = inputs[..., :half_dim]
    second = inputs[..., half_dim:]
    return jnp.concatenate(
        [first_half * cosine - second * sine_part, second * cosine + first_half * sine_part],
        axis=-1,
    )


def prompt_layout(lengths, group_rows):
    prompt_end = jnp.cumsum(lengths)
    begins = prompt_end - lengths
    position = jnp.arange(group_rows, dtype=jnp.int32)
    inside = (position[:, None] >= begins[None, :]) & (position[:, None] < prompt_end[None, :])
    starts = jnp.sum(jnp.where(inside, begins[None, :], 0), axis=1)
    return (position, starts)


def attend(query_block, key_rot, value_rows, pos_block, start_block, position):
    scores = jnp.einsum(
        "qkrd,skd->krqs", query_block, key_rot, preferred_element_type=jnp.float32
    ) * (1.0 / math.sqrt(HD))
    allowed = (position[None, :] <= pos_block[:, None]) & (
        position[None, :] >= start_block[:, None]
    )
    masked = jnp.where(allowed[None, None], scores, -jnp.inf)
    row_max = jnp.max(masked, axis=-1, keepdims=True)
    exp_scores = jnp.exp(masked - row_max)
    probs = (exp_scores / jnp.sum(exp_scores, axis=-1, keepdims=True)).astype(jnp.bfloat16)
    return jnp.einsum(
        "krqs,skd->qkrd", probs, value_rows, preferred_element_type=jnp.float32
    ).astype(jnp.bfloat16)


def local(
    tokens,
    norm_gain,
    query_gain,
    key_gain,
    w_query,
    w_key,
    w_value,
    w_out,
    prompt_lengths,
    span_group,
):
    group_rows, width_local = tokens.shape
    groups = lax.axis_size(DP)
    arrival_rows = group_rows // groups
    device_index = lax.axis_index(DP)
    block_ids = jnp.arange(groups, dtype=jnp.int32)

    own_blocks = lax.dynamic_index_in_dim(span_group, device_index, 0, keepdims=False)
    same = own_blocks[:, None] == own_blocks[None, :]
    dup_rank = jnp.sum(same & (block_ids[None, :] < block_ids[:, None]), axis=1).astype(jnp.int32)
    first_dest = jnp.where(dup_rank == 0, own_blocks, groups)
    slot_source = jnp.zeros((groups,), jnp.int32).at[first_dest].set(block_ids, mode="drop")
    dup_block = jnp.sum(jnp.where(dup_rank == 1, block_ids, 0))
    token_blocks = tokens.reshape(groups, arrival_rows, width_local)
    dup_tokens = lax.dynamic_index_in_dim(token_blocks, dup_block, 0, keepdims=False)

    weights = jnp.concatenate([w_query, w_key, w_value, w_out], axis=1)
    weight_rows, weight_width = weights.shape
    dup_size = arrival_rows * width_local
    dup_rows = -(-dup_size // weight_width)
    dup_flat = jnp.pad(dup_tokens.reshape(-1), (0, dup_rows * weight_width - dup_size))
    packed = jnp.concatenate([weights, dup_flat.reshape(dup_rows, weight_width)], axis=0)
    packed = lax.all_gather(packed, "y", axis=0, tiled=True)
    packed, token_blocks = lax.optimization_barrier((packed, token_blocks))
    packed = lax.all_gather(packed, "z", axis=0, tiled=True)
    packed = packed.reshape(groups, weight_rows + dup_rows, weight_width)
    weights = packed[:, :weight_rows].reshape(groups * weight_rows, weight_width)
    dup_all = (
        packed[:, weight_rows:]
        .reshape(groups, -1)[:, :dup_size]
        .reshape(groups, arrival_rows, width_local)
    )

    outgoing = jnp.take(token_blocks, slot_source, axis=0, mode="clip")
    incoming = lax.all_to_all(outgoing, DP, split_axis=0, concat_axis=0, tiled=True)
    counts = jnp.sum((span_group == device_index).astype(jnp.int32), axis=1)
    offsets = jnp.cumsum(counts) - counts
    first_pos = jnp.where(counts >= 1, offsets, groups)
    second_pos = jnp.where(counts == 2, offsets + 1, groups)
    source_of = (
        jnp.zeros((groups,), jnp.int32)
        .at[first_pos]
        .set(block_ids, mode="drop")
        .at[second_pos]
        .set(block_ids + groups, mode="drop")
    )
    arrived = jnp.take(incoming, source_of, axis=0, mode="clip").reshape(group_rows, width_local)
    fsdp_size = lax.axis_size("fsdp")
    spread = jnp.broadcast_to(arrived[None], (fsdp_size,) + arrived.shape)
    full_rows = lax.all_to_all(spread, "fsdp", split_axis=0, concat_axis=2, tiled=True)
    full_rows = full_rows.reshape(group_rows, width_local * fsdp_size)
    dup_source = jnp.sum(jnp.where(counts == 2, block_ids, 0))
    dup_target = jnp.sum(jnp.where(counts == 2, offsets + 1, 0))
    dup_mine = lax.dynamic_index_in_dim(dup_all, dup_source, 0, keepdims=False)
    dup_full = lax.all_gather(dup_mine, "fsdp", axis=1, tiled=True)
    full_rows = lax.dynamic_update_slice_in_dim(full_rows, dup_full, dup_target * arrival_rows, 0)
    cuts = [w_query.shape[1], w_key.shape[1], w_value.shape[1], w_out.shape[1]]
    bounds = [sum(cuts[:k]) for k in range(5)]
    query_full, key_full, value_full, out_full = (
        weights[:, bounds[k] : bounds[k + 1]] for k in range(4)
    )
    lengths = lax.dynamic_index_in_dim(prompt_lengths, device_index, 0, keepdims=False)
    position, starts = prompt_layout(lengths, group_rows)
    within = position - starts
    floats = full_rows.astype(jnp.float32)
    normed = (
        floats
        * lax.rsqrt(jnp.mean(floats * floats, axis=-1, keepdims=True) + epsilon)
        * norm_gain.astype(jnp.float32)
    ).astype(jnp.bfloat16)
    query = jnp.dot(normed, query_full, preferred_element_type=jnp.float32).reshape(
        group_rows, -1, HD
    )
    key_rows = jnp.dot(normed, key_full, preferred_element_type=jnp.float32).reshape(
        group_rows, -1, HD
    )
    value_rows = (
        jnp.dot(normed, value_full, preferred_element_type=jnp.float32)
        .reshape(group_rows, -1, HD)
        .astype(jnp.bfloat16)
    )
    query_rot = rotate(head_norm(query, query_gain), within).astype(jnp.bfloat16)
    key_rot = rotate(head_norm(key_rows, key_gain), within).astype(jnp.bfloat16)
    kv_heads = key_rot.shape[1]
    group_ratio = QH // KVH
    cache_rows = jnp.concatenate([key_rot, value_rows], axis=-1)
    block_count = group_rows // 512
    block_len = group_rows // block_count
    query_heads = query_rot.reshape(block_count, block_len, kv_heads, group_ratio, HD)

    def one_block(pieces):
        query_block, pos_block, start_block = pieces
        return attend(query_block, key_rot, value_rows, pos_block, start_block, position)

    mixed = lax.map(
        one_block,
        (
            query_heads,
            position.reshape(block_count, block_len),
            starts.reshape(block_count, block_len),
        ),
    )
    mixed = mixed.reshape(group_rows, kv_heads * group_ratio * HD)
    heads_all = lax.all_gather(mixed, "fsdp", axis=1, tiled=True)
    update = jnp.dot(heads_all, out_full, preferred_element_type=jnp.float32).astype(jnp.bfloat16)
    slot_ids = jnp.arange(2 * arrival_rows, dtype=jnp.int32)
    row_valid = slot_ids[None, :] < arrival_rows * counts[:, None]
    row_target = jnp.where(row_valid, arrival_rows * offsets[:, None] + slot_ids[None, :], 0)
    row_back = row_target.reshape(-1)
    row_mine = (
        (own_blocks * 2 + dup_rank)[:, None] * arrival_rows
        + jnp.arange(arrival_rows, dtype=jnp.int32)[None, :]
    ).reshape(-1)

    def send_back(rows):
        sent = jnp.take(rows, row_back, axis=0, mode="clip").reshape(
            (groups, 2 * arrival_rows) + rows.shape[1:]
        )
        back = lax.all_to_all(sent, DP, split_axis=0, concat_axis=0, tiled=True)
        return jnp.take(
            back.reshape((groups * 2 * arrival_rows,) + rows.shape[1:]), row_mine, axis=0, mode="clip"
        )

    cache_out = send_back(cache_rows)
    attention_out = send_back(update)
    return (attention_out, cache_out)


def solution(mesh):
    z_size = mesh.shape["dp"] // 4
    fine = Mesh(mesh.devices.reshape(z_size, 4, mesh.shape["fsdp"]), ("z", "y", "fsdp"))
    return jax.shard_map(
        local,
        mesh=fine,
        in_specs=(
            P(DP, "fsdp"),
            P(),
            P(),
            P(),
            P(DP, "fsdp"),
            P(DP, "fsdp"),
            P(DP, "fsdp"),
            P(DP, "fsdp"),
            P(),
            P(),
        ),
        out_specs=(P(DP, "fsdp"), P(DP, "fsdp", None)),
        check_vma=False,
    )
```

```python
import math

import jax
import jax.numpy as jnp
from jax import lax
from jax.sharding import Mesh, PartitionSpec as P

QH = 16
KVH = 8
HD = 128
DP = ("z", "y")


epsilon = 1e-06
rope_base = 1000000.0


def for_sending(x):

    def short(part):
        return part.astype(jnp.bfloat16) if part.dtype == jnp.float32 else part

    return jax.tree.map(short, x)


def head_norm(inputs, gains):
    inv_rms = lax.rsqrt(jnp.mean(inputs * inputs, axis=-1, keepdims=True) + epsilon)
    return inputs * inv_rms * gains.astype(jnp.float32)


def rotate(inputs, offsets):
    half_dim = inputs.shape[-1] // 2
    frequency = jnp.power(
        rope_base, -2.0 * jnp.arange(half_dim, dtype=jnp.float32) / inputs.shape[-1]
    )
    angles = offsets.astype(jnp.float32)[:, None] * frequency[None, :]
    cosine = jnp.cos(angles)[:, None, :]
    sine_part = jnp.sin(angles)[:, None, :]
    first_half = inputs[..., :half_dim]
    second = inputs[..., half_dim:]
    return jnp.concatenate(
        [first_half * cosine - second * sine_part, second * cosine + first_half * sine_part],
        axis=-1,
    )


def prompt_layout(lengths, group_rows):
    prompt_end = jnp.cumsum(lengths)
    begins = prompt_end - lengths
    position = jnp.arange(group_rows, dtype=jnp.int32)
    inside = (position[:, None] >= begins[None, :]) & (position[:, None] < prompt_end[None, :])
    starts = jnp.sum(jnp.where(inside, begins[None, :], 0), axis=1)
    return (position, starts)


def attend(query_block, key_rot, value_rows, pos_block, start_block, position):
    scores = jnp.einsum(
        "qkrd,skd->krqs", query_block, key_rot, preferred_element_type=jnp.float32
    ) * (1.0 / math.sqrt(HD))
    allowed = (position[None, :] <= pos_block[:, None]) & (
        position[None, :] >= start_block[:, None]
    )
    masked = jnp.where(allowed[None, None], scores, -jnp.inf)
    row_max = jnp.max(masked, axis=-1, keepdims=True)
    exp_scores = jnp.exp(masked - row_max)
    probs = (exp_scores / jnp.sum(exp_scores, axis=-1, keepdims=True)).astype(jnp.bfloat16)
    return jnp.einsum(
        "krqs,skd->qkrd", probs, value_rows, preferred_element_type=jnp.float32
    ).astype(jnp.bfloat16)


def local(
    tokens,
    norm_gain,
    query_gain,
    key_gain,
    w_query,
    w_key,
    w_value,
    w_out,
    prompt_lengths,
    span_group,
):
    group_rows, width_local = tokens.shape
    groups = lax.axis_size(DP)
    arrival_rows = group_rows // groups
    device_index = lax.axis_index(DP)
    block_ids = jnp.arange(groups, dtype=jnp.int32)

    own_blocks = lax.dynamic_index_in_dim(span_group, device_index, 0, keepdims=False)
    same = own_blocks[:, None] == own_blocks[None, :]
    dup_rank = jnp.sum(same & (block_ids[None, :] < block_ids[:, None]), axis=1).astype(jnp.int32)
    first_dest = jnp.where(dup_rank == 0, own_blocks, groups)
    slot_source = jnp.zeros((groups,), jnp.int32).at[first_dest].set(block_ids, mode="drop")
    dup_block = jnp.sum(jnp.where(dup_rank == 1, block_ids, 0))
    token_blocks = tokens.reshape(groups, arrival_rows, width_local)
    dup_tokens = lax.dynamic_index_in_dim(token_blocks, dup_block, 0, keepdims=False)

    weights = jnp.concatenate([w_query, w_key, w_value, w_out], axis=1)
    weight_rows, weight_width = weights.shape
    packed = jnp.concatenate([weights, dup_tokens.reshape(weight_rows, -1)], axis=1)
    packed = lax.all_gather(packed, "y", axis=0, tiled=True)
    packed, token_blocks = lax.optimization_barrier((packed, token_blocks))
    packed = lax.all_gather(packed, "z", axis=0, tiled=True)
    weights = packed[:, :weight_width]
    dup_all = packed[:, weight_width:].reshape(groups, arrival_rows, width_local)

    outgoing = jnp.take(token_blocks, slot_source, axis=0, mode="clip")
    incoming = lax.all_to_all(outgoing, DP, split_axis=0, concat_axis=0, tiled=True)
    counts = jnp.sum((span_group == device_index).astype(jnp.int32), axis=1)
    offsets = jnp.cumsum(counts) - counts
    first_pos = jnp.where(counts >= 1, offsets, groups)
    second_pos = jnp.where(counts == 2, offsets + 1, groups)
    source_of = (
        jnp.zeros((groups,), jnp.int32)
        .at[first_pos]
        .set(block_ids, mode="drop")
        .at[second_pos]
        .set(block_ids + groups, mode="drop")
    )
    arrived = jnp.take(incoming, source_of, axis=0, mode="clip").reshape(group_rows, width_local)
    fsdp_size = lax.axis_size("fsdp")
    spread = jnp.broadcast_to(arrived[None], (fsdp_size,) + arrived.shape)
    pieces = lax.all_to_all(spread, "fsdp", split_axis=0, concat_axis=0, tiled=True)
    dup_source = jnp.sum(jnp.where(counts == 2, block_ids, 0))
    dup_target = jnp.sum(jnp.where(counts == 2, offsets + 1, 0))
    dup_mine = lax.dynamic_index_in_dim(dup_all, dup_source, 0, keepdims=False)
    dup_pieces = lax.all_gather(dup_mine, "fsdp", axis=0, tiled=False)
    pieces = lax.dynamic_update_slice_in_dim(pieces, dup_pieces, dup_target * arrival_rows, 1)
    cuts = [w_query.shape[1], w_key.shape[1], w_value.shape[1], w_out.shape[1]]
    bounds = [sum(cuts[:k]) for k in range(5)]
    query_full, key_full, value_full, out_full = (
        weights[:, bounds[k] : bounds[k + 1]] for k in range(4)
    )
    lengths = lax.dynamic_index_in_dim(prompt_lengths, device_index, 0, keepdims=False)
    position, starts = prompt_layout(lengths, group_rows)
    within = position - starts
    floats = pieces.astype(jnp.float32)
    normed = (
        floats
        * lax.rsqrt(jnp.mean(floats * floats, axis=(0, 2), keepdims=True) + epsilon)
        * norm_gain.astype(jnp.float32).reshape(fsdp_size, 1, width_local)
    ).astype(jnp.bfloat16)

    def project(matrix):
        return jnp.einsum(
            "fnk,fkc->nc",
            normed,
            matrix.reshape(fsdp_size, width_local, -1),
            preferred_element_type=jnp.float32,
        )

    query = project(query_full).reshape(group_rows, -1, HD)
    key_rows = project(key_full).reshape(group_rows, -1, HD)
    value_rows = project(value_full).reshape(group_rows, -1, HD).astype(jnp.bfloat16)
    query_rot = rotate(head_norm(query, query_gain), within).astype(jnp.bfloat16)
    key_rot = rotate(head_norm(key_rows, key_gain), within).astype(jnp.bfloat16)
    kv_heads = key_rot.shape[1]
    group_ratio = QH // KVH
    cache_rows = jnp.concatenate([key_rot, value_rows], axis=-1)
    block_count = group_rows // 512
    block_len = group_rows // block_count
    query_heads = query_rot.reshape(block_count, block_len, kv_heads, group_ratio, HD)

    def one_block(pieces):
        query_block, pos_block, start_block = pieces
        return attend(query_block, key_rot, value_rows, pos_block, start_block, position)

    mixed = lax.map(
        one_block,
        (
            query_heads,
            position.reshape(block_count, block_len),
            starts.reshape(block_count, block_len),
        ),
    )
    mixed = mixed.reshape(group_rows, kv_heads * group_ratio * HD)
    heads_all = lax.all_gather(mixed, "fsdp", axis=1, tiled=True)
    update = jnp.dot(heads_all, out_full, preferred_element_type=jnp.float32).astype(jnp.bfloat16)
    sub_ids = jnp.arange(2, dtype=jnp.int32)
    block_back = jnp.where(
        sub_ids[None, :] < counts[:, None], offsets[:, None] + sub_ids[None, :], 0
    ).reshape(-1)
    block_mine = own_blocks * 2 + dup_rank

    def send_back(rows):
        tail = rows.shape[1:]
        sent = jnp.take(
            rows.reshape((groups, arrival_rows) + tail), block_back, axis=0, mode="clip"
        ).reshape((groups, 2 * arrival_rows) + tail)
        back = lax.all_to_all(sent, DP, split_axis=0, concat_axis=0, tiled=True)
        return jnp.take(
            back.reshape((groups * 2, arrival_rows) + tail), block_mine, axis=0, mode="clip"
        ).reshape(rows.shape)
    cache_out = send_back(cache_rows)
    attention_out = send_back(update)
    return (attention_out, cache_out)


def solution(mesh):
    z_size = mesh.shape["dp"] // 4
    fine = Mesh(mesh.devices.reshape(z_size, 4, mesh.shape["fsdp"]), ("z", "y", "fsdp"))
    return jax.shard_map(
        local,
        mesh=fine,
        in_specs=(
            P(DP, "fsdp"),
            P(),
            P(),
            P(),
            P(DP, "fsdp"),
            P(DP, "fsdp"),
            P(DP, "fsdp"),
            P(DP, "fsdp"),
            P(),
            P(),
        ),
        out_specs=(P(DP, "fsdp"), P(DP, "fsdp", None)),
        check_vma=False,
    )
```

```python
import math

import jax
import jax.numpy as jnp
from jax import lax
from jax.sharding import Mesh, PartitionSpec as P

QH = 16
KVH = 8
HD = 128
DP = ("z", "y")


epsilon = 1e-06
rope_base = 1000000.0


def for_sending(x):

    def short(part):
        return part.astype(jnp.bfloat16) if part.dtype == jnp.float32 else part

    return jax.tree.map(short, x)


def head_norm(inputs, gains):
    inv_rms = lax.rsqrt(jnp.mean(inputs * inputs, axis=-1, keepdims=True) + epsilon)
    return inputs * inv_rms * gains.astype(jnp.float32)


def rotate(inputs, offsets):
    half_dim = inputs.shape[-1] // 2
    frequency = jnp.power(
        rope_base, -2.0 * jnp.arange(half_dim, dtype=jnp.float32) / inputs.shape[-1]
    )
    angles = offsets.astype(jnp.float32)[:, None] * frequency[None, :]
    cosine = jnp.cos(angles)[:, None, :]
    sine_part = jnp.sin(angles)[:, None, :]
    first_half = inputs[..., :half_dim]
    second = inputs[..., half_dim:]
    return jnp.concatenate(
        [first_half * cosine - second * sine_part, second * cosine + first_half * sine_part],
        axis=-1,
    )


def prompt_layout(lengths, group_rows):
    prompt_end = jnp.cumsum(lengths)
    begins = prompt_end - lengths
    position = jnp.arange(group_rows, dtype=jnp.int32)
    inside = (position[:, None] >= begins[None, :]) & (position[:, None] < prompt_end[None, :])
    starts = jnp.sum(jnp.where(inside, begins[None, :], 0), axis=1)
    return (position, starts)


def attend(query_block, key_rot, value_rows, pos_block, start_block, position):
    scores = jnp.einsum(
        "qkrd,skd->krqs", query_block, key_rot, preferred_element_type=jnp.float32
    ) * (1.0 / math.sqrt(HD))
    allowed = (position[None, :] <= pos_block[:, None]) & (
        position[None, :] >= start_block[:, None]
    )
    masked = jnp.where(allowed[None, None], scores, -jnp.inf)
    row_max = jnp.max(masked, axis=-1, keepdims=True)
    exp_scores = jnp.exp(masked - row_max)
    probs = (exp_scores / jnp.sum(exp_scores, axis=-1, keepdims=True)).astype(jnp.bfloat16)
    return jnp.einsum(
        "krqs,skd->qkrd", probs, value_rows, preferred_element_type=jnp.float32
    ).astype(jnp.bfloat16)


def local(
    tokens,
    norm_gain,
    query_gain,
    key_gain,
    w_query,
    w_key,
    w_value,
    w_out,
    prompt_lengths,
    span_group,
):
    group_rows, width_local = tokens.shape
    groups = lax.axis_size(DP)
    arrival_rows = group_rows // groups
    device_index = lax.axis_index(DP)
    block_ids = jnp.arange(groups, dtype=jnp.int32)

    own_blocks = lax.dynamic_index_in_dim(span_group, device_index, 0, keepdims=False)
    same = own_blocks[:, None] == own_blocks[None, :]
    dup_rank = jnp.sum(same & (block_ids[None, :] < block_ids[:, None]), axis=1).astype(jnp.int32)
    first_dest = jnp.where(dup_rank == 0, own_blocks, groups)
    slot_source = jnp.zeros((groups,), jnp.int32).at[first_dest].set(block_ids, mode="drop")
    dup_block = jnp.sum(jnp.where(dup_rank == 1, block_ids, 0))
    token_blocks = tokens.reshape(groups, arrival_rows, width_local)
    dup_tokens = lax.dynamic_index_in_dim(token_blocks, dup_block, 0, keepdims=False)

    weights = jnp.concatenate([w_query, w_key, w_value, w_out], axis=1)
    weight_rows, weight_width = weights.shape
    packed = jnp.concatenate([weights, dup_tokens.reshape(weight_rows, -1)], axis=1)
    packed = lax.all_gather(packed, "y", axis=0, tiled=True)
    packed, token_blocks = lax.optimization_barrier((packed, token_blocks))
    packed = lax.all_gather(packed, "z", axis=0, tiled=True)
    weights = packed[:, :weight_width]
    dup_all = packed[:, weight_width:].reshape(groups, arrival_rows, width_local)

    outgoing = jnp.take(token_blocks, slot_source, axis=0, mode="clip")
    incoming = lax.all_to_all(outgoing, DP, split_axis=0, concat_axis=0, tiled=True)
    counts = jnp.sum((span_group == device_index).astype(jnp.int32), axis=1)
    offsets = jnp.cumsum(counts) - counts
    first_pos = jnp.where(counts >= 1, offsets, groups)
    second_pos = jnp.where(counts == 2, offsets + 1, groups)
    source_of = (
        jnp.zeros((groups,), jnp.int32)
        .at[first_pos]
        .set(block_ids, mode="drop")
        .at[second_pos]
        .set(block_ids + groups, mode="drop")
    )
    arrived = jnp.take(incoming, source_of, axis=0, mode="clip").reshape(group_rows, width_local)
    fsdp_size = lax.axis_size("fsdp")
    spread = jnp.broadcast_to(arrived[None], (fsdp_size,) + arrived.shape)
    pieces = lax.all_to_all(spread, "fsdp", split_axis=0, concat_axis=0, tiled=True)
    dup_source = jnp.sum(jnp.where(counts == 2, block_ids, 0))
    dup_target = jnp.sum(jnp.where(counts == 2, offsets + 1, 0))
    dup_mine = lax.dynamic_index_in_dim(dup_all, dup_source, 0, keepdims=False)
    dup_spread = jnp.broadcast_to(dup_mine[None], (fsdp_size,) + dup_mine.shape)
    dup_pieces = lax.all_to_all(dup_spread, "fsdp", split_axis=0, concat_axis=0, tiled=True)
    cuts = [w_query.shape[1], w_key.shape[1], w_value.shape[1], w_out.shape[1]]
    bounds = [sum(cuts[:k]) for k in range(5)]
    query_full, key_full, value_full, out_full = (
        weights[:, bounds[k] : bounds[k + 1]] for k in range(4)
    )
    lengths = lax.dynamic_index_in_dim(prompt_lengths, device_index, 0, keepdims=False)
    position, starts = prompt_layout(lengths, group_rows)
    within = position - starts
    def normalize(parts):
        floats = parts.astype(jnp.float32)
        return (
            floats
            * lax.rsqrt(jnp.mean(floats * floats, axis=(0, 2), keepdims=True) + epsilon)
            * norm_gain.astype(jnp.float32).reshape(fsdp_size, 1, width_local)
        ).astype(jnp.bfloat16)

    def project(normed, matrix):
        return jnp.einsum(
            "fnk,fkc->nc",
            normed,
            matrix.reshape(fsdp_size, width_local, -1),
            preferred_element_type=jnp.float32,
        )

    def with_dup(matrix):
        main = project(normed_main, matrix)
        extra = project(normed_dup, matrix)
        return lax.dynamic_update_slice_in_dim(main, extra, dup_target * arrival_rows, 0)

    normed_main = normalize(pieces)
    normed_dup = normalize(dup_pieces)
    query = with_dup(query_full).reshape(group_rows, -1, HD)
    key_rows = with_dup(key_full).reshape(group_rows, -1, HD)
    value_rows = with_dup(value_full).reshape(group_rows, -1, HD).astype(jnp.bfloat16)
    query_rot = rotate(head_norm(query, query_gain), within).astype(jnp.bfloat16)
    key_rot = rotate(head_norm(key_rows, key_gain), within).astype(jnp.bfloat16)
    kv_heads = key_rot.shape[1]
    group_ratio = QH // KVH
    cache_rows = jnp.concatenate([key_rot, value_rows], axis=-1)
    block_count = group_rows // 512
    block_len = group_rows // block_count
    query_heads = query_rot.reshape(block_count, block_len, kv_heads, group_ratio, HD)

    def one_block(pieces):
        query_block, pos_block, start_block = pieces
        return attend(query_block, key_rot, value_rows, pos_block, start_block, position)

    mixed = lax.map(
        one_block,
        (
            query_heads,
            position.reshape(block_count, block_len),
            starts.reshape(block_count, block_len),
        ),
    )
    mixed = mixed.reshape(group_rows, kv_heads * group_ratio * HD)
    heads_all = lax.all_gather(mixed, "fsdp", axis=1, tiled=True)
    update = jnp.dot(heads_all, out_full, preferred_element_type=jnp.float32).astype(jnp.bfloat16)
    sub_ids = jnp.arange(2, dtype=jnp.int32)
    block_back = jnp.where(
        sub_ids[None, :] < counts[:, None], offsets[:, None] + sub_ids[None, :], 0
    ).reshape(-1)
    block_mine = own_blocks * 2 + dup_rank

    def send_back(rows):
        tail = rows.shape[1:]
        sent = jnp.take(
            rows.reshape((groups, arrival_rows) + tail), block_back, axis=0, mode="clip"
        ).reshape((groups, 2 * arrival_rows) + tail)
        back = lax.all_to_all(sent, DP, split_axis=0, concat_axis=0, tiled=True)
        return jnp.take(
            back.reshape((groups * 2, arrival_rows) + tail), block_mine, axis=0, mode="clip"
        ).reshape(rows.shape)
    cache_out = send_back(cache_rows)
    attention_out = send_back(update)
    return (attention_out, cache_out)


def solution(mesh):
    z_size = mesh.shape["dp"] // 4
    fine = Mesh(mesh.devices.reshape(z_size, 4, mesh.shape["fsdp"]), ("z", "y", "fsdp"))
    return jax.shard_map(
        local,
        mesh=fine,
        in_specs=(
            P(DP, "fsdp"),
            P(),
            P(),
            P(),
            P(DP, "fsdp"),
            P(DP, "fsdp"),
            P(DP, "fsdp"),
            P(DP, "fsdp"),
            P(),
            P(),
        ),
        out_specs=(P(DP, "fsdp"), P(DP, "fsdp", None)),
        check_vma=False,
    )
```

```python
import math

import jax
import jax.numpy as jnp
from jax import lax
from jax.sharding import Mesh, PartitionSpec as P

QH = 16
KVH = 8
HD = 128
DP = ("z", "y")


epsilon = 1e-06
rope_base = 1000000.0


def for_sending(x):

    def short(part):
        return part.astype(jnp.bfloat16) if part.dtype == jnp.float32 else part

    return jax.tree.map(short, x)


def head_norm(inputs, gains):
    inv_rms = lax.rsqrt(jnp.mean(inputs * inputs, axis=-1, keepdims=True) + epsilon)
    return inputs * inv_rms * gains.astype(jnp.float32)


def rotate(inputs, offsets):
    half_dim = inputs.shape[-1] // 2
    frequency = jnp.power(
        rope_base, -2.0 * jnp.arange(half_dim, dtype=jnp.float32) / inputs.shape[-1]
    )
    angles = offsets.astype(jnp.float32)[:, None] * frequency[None, :]
    cosine = jnp.cos(angles)[:, None, :]
    sine_part = jnp.sin(angles)[:, None, :]
    first_half = inputs[..., :half_dim]
    second = inputs[..., half_dim:]
    return jnp.concatenate(
        [first_half * cosine - second * sine_part, second * cosine + first_half * sine_part],
        axis=-1,
    )


def prompt_layout(lengths, group_rows):
    prompt_end = jnp.cumsum(lengths)
    begins = prompt_end - lengths
    position = jnp.arange(group_rows, dtype=jnp.int32)
    inside = (position[:, None] >= begins[None, :]) & (position[:, None] < prompt_end[None, :])
    starts = jnp.sum(jnp.where(inside, begins[None, :], 0), axis=1)
    return (position, starts)


def attend(query_block, key_rot, value_rows, pos_block, start_block, position):
    scores = jnp.einsum(
        "qkrd,skd->krqs", query_block, key_rot, preferred_element_type=jnp.float32
    ) * (1.0 / math.sqrt(HD))
    allowed = (position[None, :] <= pos_block[:, None]) & (
        position[None, :] >= start_block[:, None]
    )
    masked = jnp.where(allowed[None, None], scores, -jnp.inf)
    row_max = jnp.max(masked, axis=-1, keepdims=True)
    exp_scores = jnp.exp(masked - row_max)
    probs = (exp_scores / jnp.sum(exp_scores, axis=-1, keepdims=True)).astype(jnp.bfloat16)
    return jnp.einsum(
        "krqs,skd->qkrd", probs, value_rows, preferred_element_type=jnp.float32
    ).astype(jnp.bfloat16)


def local(
    tokens,
    norm_gain,
    query_gain,
    key_gain,
    w_query,
    w_key,
    w_value,
    w_out,
    prompt_lengths,
    span_group,
):
    group_rows, width_local = tokens.shape
    groups = lax.axis_size(DP)
    arrival_rows = group_rows // groups
    device_index = lax.axis_index(DP)
    block_ids = jnp.arange(groups, dtype=jnp.int32)

    own_blocks = lax.dynamic_index_in_dim(span_group, device_index, 0, keepdims=False)
    same = own_blocks[:, None] == own_blocks[None, :]
    dup_rank = jnp.sum(same & (block_ids[None, :] < block_ids[:, None]), axis=1).astype(jnp.int32)
    first_dest = jnp.where(dup_rank == 0, own_blocks, groups)
    slot_source = jnp.zeros((groups,), jnp.int32).at[first_dest].set(block_ids, mode="drop")
    dup_block = jnp.sum(jnp.where(dup_rank == 1, block_ids, 0))
    token_blocks = tokens.reshape(groups, arrival_rows, width_local)
    dup_tokens = lax.dynamic_index_in_dim(token_blocks, dup_block, 0, keepdims=False)

    weights = jnp.concatenate([w_query, w_key, w_value, w_out], axis=1)
    weight_rows, weight_width = weights.shape
    packed = jnp.concatenate([weights, dup_tokens.reshape(weight_rows, -1)], axis=1)
    packed = lax.all_gather(packed, "y", axis=0, tiled=True)
    packed, token_blocks = lax.optimization_barrier((packed, token_blocks))
    packed = lax.all_gather(packed, "z", axis=0, tiled=True)
    weights = packed[:, :weight_width]
    dup_all = packed[:, weight_width:].reshape(groups, arrival_rows, width_local)

    outgoing = jnp.take(token_blocks, slot_source, axis=0, mode="clip")
    incoming = lax.all_to_all(outgoing, DP, split_axis=0, concat_axis=0, tiled=True)
    counts = jnp.sum((span_group == device_index).astype(jnp.int32), axis=1)
    offsets = jnp.cumsum(counts) - counts
    first_pos = jnp.where(counts >= 1, offsets, groups)
    second_pos = jnp.where(counts == 2, offsets + 1, groups)
    source_of = (
        jnp.zeros((groups,), jnp.int32)
        .at[first_pos]
        .set(block_ids, mode="drop")
        .at[second_pos]
        .set(block_ids + groups, mode="drop")
    )
    arrived = jnp.take(incoming, source_of, axis=0, mode="clip").reshape(group_rows, width_local)
    fsdp_size = lax.axis_size("fsdp")
    spread = jnp.broadcast_to(arrived[None], (fsdp_size,) + arrived.shape)
    pieces = lax.all_to_all(spread, "fsdp", split_axis=0, concat_axis=0, tiled=True)
    dup_source = jnp.sum(jnp.where(counts == 2, block_ids, 0))
    dup_target = jnp.sum(jnp.where(counts == 2, offsets + 1, 0))
    dup_mine = lax.dynamic_index_in_dim(dup_all, dup_source, 0, keepdims=False)
    dup_pieces = lax.all_gather(dup_mine, "fsdp", axis=0, tiled=False)
    pieces = lax.dynamic_update_slice_in_dim(pieces, dup_pieces, dup_target * arrival_rows, 1)
    sub_ids = jnp.arange(2, dtype=jnp.int32)
    block_back = jnp.where(
        sub_ids[None, :] < counts[:, None], offsets[:, None] + sub_ids[None, :], 0
    ).reshape(-1)
    block_mine = own_blocks * 2 + dup_rank

    def send_back(blocks):
        rows = blocks.shape[1]
        tail = blocks.shape[2:]
        sent = jnp.take(blocks, block_back, axis=0, mode="clip").reshape(
            (groups, 2 * rows) + tail
        )
        back = lax.all_to_all(sent, DP, split_axis=0, concat_axis=0, tiled=True)
        return jnp.take(
            back.reshape((groups * 2, rows) + tail), block_mine, axis=0, mode="clip"
        )
    cuts = [w_query.shape[1], w_key.shape[1], w_value.shape[1], w_out.shape[1]]
    bounds = [sum(cuts[:k]) for k in range(5)]
    query_full, key_full, value_full, out_full = (
        weights[:, bounds[k] : bounds[k + 1]] for k in range(4)
    )
    lengths = lax.dynamic_index_in_dim(prompt_lengths, device_index, 0, keepdims=False)
    position, starts = prompt_layout(lengths, group_rows)
    within = position - starts
    floats = pieces.astype(jnp.float32)
    normed = (
        floats
        * lax.rsqrt(jnp.mean(floats * floats, axis=(0, 2), keepdims=True) + epsilon)
        * norm_gain.astype(jnp.float32).reshape(fsdp_size, 1, width_local)
    ).astype(jnp.bfloat16)

    def project(matrix):
        return jnp.einsum(
            "fnk,fkc->nc",
            normed,
            matrix.reshape(fsdp_size, width_local, -1),
            preferred_element_type=jnp.float32,
        )

    query = project(query_full).reshape(group_rows, -1, HD)
    key_rows = project(key_full).reshape(group_rows, -1, HD)
    value_rows = project(value_full).reshape(group_rows, -1, HD).astype(jnp.bfloat16)
    query_rot = rotate(head_norm(query, query_gain), within).astype(jnp.bfloat16)
    key_rot = rotate(head_norm(key_rows, key_gain), within).astype(jnp.bfloat16)
    kv_heads = key_rot.shape[1]
    group_ratio = QH // KVH
    cache_rows = jnp.concatenate([key_rot, value_rows], axis=-1)
    block_count = group_rows // 512
    block_len = group_rows // block_count
    query_heads = query_rot.reshape(block_count, block_len, kv_heads, group_ratio, HD)

    def one_block(pieces):
        query_block, pos_block, start_block = pieces
        return attend(query_block, key_rot, value_rows, pos_block, start_block, position)

    mixed = lax.map(
        one_block,
        (
            query_heads,
            position.reshape(block_count, block_len),
            starts.reshape(block_count, block_len),
        ),
    )
    half_rows = arrival_rows // 2
    mixed = mixed.reshape(groups, 2, half_rows, kv_heads * group_ratio * HD)
    update_halves = []
    for half in range(2):
        heads_half = lax.all_gather(
            mixed[:, half].reshape(groups * half_rows, -1), "fsdp", axis=1, tiled=True
        )
        update_half = jnp.dot(
            heads_half, out_full, preferred_element_type=jnp.float32
        ).astype(jnp.bfloat16)
        update_halves.append(send_back(update_half.reshape(groups, half_rows, -1)))
    attention_out = jnp.stack(update_halves, axis=1).reshape(group_rows, -1)
    cache_out = send_back(cache_rows.reshape((groups, arrival_rows) + cache_rows.shape[1:])).reshape(cache_rows.shape)
    return (attention_out, cache_out)


def solution(mesh):
    z_size = mesh.shape["dp"] // 4
    fine = Mesh(mesh.devices.reshape(z_size, 4, mesh.shape["fsdp"]), ("z", "y", "fsdp"))
    return jax.shard_map(
        local,
        mesh=fine,
        in_specs=(
            P(DP, "fsdp"),
            P(),
            P(),
            P(),
            P(DP, "fsdp"),
            P(DP, "fsdp"),
            P(DP, "fsdp"),
            P(DP, "fsdp"),
            P(),
            P(),
        ),
        out_specs=(P(DP, "fsdp"), P(DP, "fsdp", None)),
        check_vma=False,
    )
```

```python
import math

import jax
import jax.numpy as jnp
from jax import lax
from jax.sharding import Mesh, PartitionSpec as P

QH = 16
KVH = 8
HD = 128
DP = ("z", "y")


epsilon = 1e-06
rope_base = 1000000.0


def for_sending(x):

    def short(part):
        return part.astype(jnp.bfloat16) if part.dtype == jnp.float32 else part

    return jax.tree.map(short, x)


def head_norm(inputs, gains):
    inv_rms = lax.rsqrt(jnp.mean(inputs * inputs, axis=-1, keepdims=True) + epsilon)
    return inputs * inv_rms * gains.astype(jnp.float32)


def rotate(inputs, offsets):
    half_dim = inputs.shape[-1] // 2
    frequency = jnp.power(
        rope_base, -2.0 * jnp.arange(half_dim, dtype=jnp.float32) / inputs.shape[-1]
    )
    angles = offsets.astype(jnp.float32)[:, None] * frequency[None, :]
    cosine = jnp.cos(angles)[:, None, :]
    sine_part = jnp.sin(angles)[:, None, :]
    first_half = inputs[..., :half_dim]
    second = inputs[..., half_dim:]
    return jnp.concatenate(
        [first_half * cosine - second * sine_part, second * cosine + first_half * sine_part],
        axis=-1,
    )


def prompt_layout(lengths, group_rows):
    prompt_end = jnp.cumsum(lengths)
    begins = prompt_end - lengths
    position = jnp.arange(group_rows, dtype=jnp.int32)
    inside = (position[:, None] >= begins[None, :]) & (position[:, None] < prompt_end[None, :])
    starts = jnp.sum(jnp.where(inside, begins[None, :], 0), axis=1)
    return (position, starts)


def attend(query_block, key_rot, value_rows, pos_block, start_block, position):
    scores = jnp.einsum(
        "qkrd,skd->krqs", query_block, key_rot, preferred_element_type=jnp.float32
    ) * (1.0 / math.sqrt(HD))
    allowed = (position[None, :] <= pos_block[:, None]) & (
        position[None, :] >= start_block[:, None]
    )
    masked = jnp.where(allowed[None, None], scores, -jnp.inf)
    row_max = jnp.max(masked, axis=-1, keepdims=True)
    exp_scores = jnp.exp(masked - row_max)
    probs = (exp_scores / jnp.sum(exp_scores, axis=-1, keepdims=True)).astype(jnp.bfloat16)
    return jnp.einsum(
        "krqs,skd->qkrd", probs, value_rows, preferred_element_type=jnp.float32
    ).astype(jnp.bfloat16)


def local(
    tokens,
    norm_gain,
    query_gain,
    key_gain,
    w_query,
    w_key,
    w_value,
    w_out,
    prompt_lengths,
    span_group,
):
    group_rows, width_local = tokens.shape
    groups = lax.axis_size(DP)
    arrival_rows = group_rows // groups
    device_index = lax.axis_index(DP)
    block_ids = jnp.arange(groups, dtype=jnp.int32)

    own_blocks = lax.dynamic_index_in_dim(span_group, device_index, 0, keepdims=False)
    same = own_blocks[:, None] == own_blocks[None, :]
    dup_rank = jnp.sum(same & (block_ids[None, :] < block_ids[:, None]), axis=1).astype(jnp.int32)
    first_dest = jnp.where(dup_rank == 0, own_blocks, groups)
    slot_source = jnp.zeros((groups,), jnp.int32).at[first_dest].set(block_ids, mode="drop")
    dup_block = jnp.sum(jnp.where(dup_rank == 1, block_ids, 0))
    token_blocks = tokens.reshape(groups, arrival_rows, width_local)
    dup_tokens = lax.dynamic_index_in_dim(token_blocks, dup_block, 0, keepdims=False)

    weights = jnp.concatenate([w_query, w_key, w_value, w_out], axis=1)
    weight_rows, weight_width = weights.shape
    packed = jnp.concatenate([weights, dup_tokens.reshape(weight_rows, -1)], axis=1)
    packed = lax.all_gather(packed, "y", axis=0, tiled=True)
    packed, token_blocks = lax.optimization_barrier((packed, token_blocks))
    packed = lax.all_gather(packed, "z", axis=0, tiled=True)
    weights = packed[:, :weight_width]
    dup_all = packed[:, weight_width:].reshape(groups, arrival_rows, width_local)

    outgoing = jnp.take(token_blocks, slot_source, axis=0, mode="clip")
    incoming = lax.all_to_all(outgoing, DP, split_axis=0, concat_axis=0, tiled=True)
    counts = jnp.sum((span_group == device_index).astype(jnp.int32), axis=1)
    offsets = jnp.cumsum(counts) - counts
    first_pos = jnp.where(counts >= 1, offsets, groups)
    second_pos = jnp.where(counts == 2, offsets + 1, groups)
    source_of = (
        jnp.zeros((groups,), jnp.int32)
        .at[first_pos]
        .set(block_ids, mode="drop")
        .at[second_pos]
        .set(block_ids + groups, mode="drop")
    )
    arrived = jnp.take(incoming, source_of, axis=0, mode="clip").reshape(group_rows, width_local)
    fsdp_size = lax.axis_size("fsdp")
    spread = jnp.broadcast_to(arrived[None], (fsdp_size,) + arrived.shape)
    pieces = lax.all_to_all(spread, "fsdp", split_axis=0, concat_axis=0, tiled=True)
    dup_source = jnp.sum(jnp.where(counts == 2, block_ids, 0))
    dup_target = jnp.sum(jnp.where(counts == 2, offsets + 1, 0))
    dup_mine = lax.dynamic_index_in_dim(dup_all, dup_source, 0, keepdims=False)
    dup_pieces = lax.all_gather(dup_mine, "fsdp", axis=0, tiled=False)
    pieces = lax.dynamic_update_slice_in_dim(pieces, dup_pieces, dup_target * arrival_rows, 1)
    cuts = [w_query.shape[1], w_key.shape[1], w_value.shape[1], w_out.shape[1]]
    bounds = [sum(cuts[:k]) for k in range(5)]
    query_full, key_full, value_full, out_full = (
        weights[:, bounds[k] : bounds[k + 1]] for k in range(4)
    )
    lengths = lax.dynamic_index_in_dim(prompt_lengths, device_index, 0, keepdims=False)
    position, starts = prompt_layout(lengths, group_rows)
    within = position - starts
    floats = pieces.astype(jnp.float32)
    normed = (
        floats
        * lax.rsqrt(jnp.mean(floats * floats, axis=(0, 2), keepdims=True) + epsilon)
        * norm_gain.astype(jnp.float32).reshape(fsdp_size, 1, width_local)
    ).astype(jnp.bfloat16)

    def project(matrix):
        return jnp.einsum(
            "fnk,fkc->nc",
            normed,
            matrix.reshape(fsdp_size, width_local, -1),
            preferred_element_type=jnp.float32,
        )

    query = project(query_full).reshape(group_rows, -1, HD)
    key_rows = project(key_full).reshape(group_rows, -1, HD)
    value_rows = project(value_full).reshape(group_rows, -1, HD).astype(jnp.bfloat16)
    query_rot = rotate(head_norm(query, query_gain), within).astype(jnp.bfloat16)
    key_rot = rotate(head_norm(key_rows, key_gain), within).astype(jnp.bfloat16)
    kv_heads = key_rot.shape[1]
    group_ratio = QH // KVH
    cache_rows = jnp.concatenate([key_rot, value_rows], axis=-1)
    block_count = group_rows // 512
    block_len = group_rows // block_count
    query_heads = query_rot.reshape(block_count, block_len, kv_heads, group_ratio, HD)

    def one_block(pieces):
        query_block, pos_block, start_block = pieces
        return attend(query_block, key_rot, value_rows, pos_block, start_block, position)

    mixed = lax.map(
        one_block,
        (
            query_heads,
            position.reshape(block_count, block_len),
            starts.reshape(block_count, block_len),
        ),
    )
    mixed = mixed.reshape(group_rows, kv_heads * group_ratio * HD)
    heads_all = lax.all_gather(mixed, "fsdp", axis=1, tiled=True)
    cache_blocks = cache_rows.reshape((groups, arrival_rows) + cache_rows.shape[1:])
    dup_position = jnp.sum(jnp.where(counts == 2, offsets + 1, 0))
    dup_cache = lax.dynamic_index_in_dim(cache_blocks, dup_position, 0, keepdims=True)
    dup_cache, heads_all = lax.optimization_barrier((dup_cache, heads_all))
    dup_cache = lax.all_gather(dup_cache, "y", axis=0, tiled=True)
    dup_cache = lax.all_gather(dup_cache, "z", axis=0, tiled=True)
    update = jnp.dot(heads_all, out_full, preferred_element_type=jnp.float32).astype(jnp.bfloat16)
    sub_ids = jnp.arange(2, dtype=jnp.int32)
    block_back = jnp.where(
        sub_ids[None, :] < counts[:, None], offsets[:, None] + sub_ids[None, :], 0
    ).reshape(-1)
    block_mine = own_blocks * 2 + dup_rank

    def send_back(rows):
        tail = rows.shape[1:]
        sent = jnp.take(
            rows.reshape((groups, arrival_rows) + tail), block_back, axis=0, mode="clip"
        ).reshape((groups, 2 * arrival_rows) + tail)
        back = lax.all_to_all(sent, DP, split_axis=0, concat_axis=0, tiled=True)
        return jnp.take(
            back.reshape((groups * 2, arrival_rows) + tail), block_mine, axis=0, mode="clip"
        ).reshape(rows.shape)
    sent_cache = jnp.take(cache_blocks, offsets, axis=0, mode="clip")
    back_cache = lax.all_to_all(sent_cache, DP, split_axis=0, concat_axis=0, tiled=True)
    cache_out = jnp.take(
        jnp.concatenate([back_cache, dup_cache], axis=0),
        own_blocks + groups * dup_rank,
        axis=0,
        mode="clip",
    ).reshape(cache_rows.shape)
    attention_out = send_back(update)
    return (attention_out, cache_out)


def solution(mesh):
    z_size = mesh.shape["dp"] // 4
    fine = Mesh(mesh.devices.reshape(z_size, 4, mesh.shape["fsdp"]), ("z", "y", "fsdp"))
    return jax.shard_map(
        local,
        mesh=fine,
        in_specs=(
            P(DP, "fsdp"),
            P(),
            P(),
            P(),
            P(DP, "fsdp"),
            P(DP, "fsdp"),
            P(DP, "fsdp"),
            P(DP, "fsdp"),
            P(),
            P(),
        ),
        out_specs=(P(DP, "fsdp"), P(DP, "fsdp", None)),
        check_vma=False,
    )
```

```python
import math

import jax
import jax.numpy as jnp
from jax import lax
from jax.sharding import Mesh, PartitionSpec as P

QH = 16
KVH = 8
HD = 128
DP = ("z", "y")


epsilon = 1e-06
rope_base = 1000000.0


def head_norm(inputs, gains):
    inv_rms = lax.rsqrt(jnp.mean(inputs * inputs, axis=-1, keepdims=True) + epsilon)
    return inputs * inv_rms * gains.astype(jnp.float32)


def rotate(inputs, offsets):
    half_dim = inputs.shape[-1] // 2
    frequency = jnp.power(
        rope_base, -2.0 * jnp.arange(half_dim, dtype=jnp.float32) / inputs.shape[-1]
    )
    angles = offsets.astype(jnp.float32)[:, None] * frequency[None, :]
    cosine = jnp.cos(angles)[:, None, :]
    sine_part = jnp.sin(angles)[:, None, :]
    first_half = inputs[..., :half_dim]
    second = inputs[..., half_dim:]
    return jnp.concatenate(
        [first_half * cosine - second * sine_part, second * cosine + first_half * sine_part],
        axis=-1,
    )


def prompt_layout(lengths, group_rows):
    prompt_end = jnp.cumsum(lengths)
    begins = prompt_end - lengths
    position = jnp.arange(group_rows, dtype=jnp.int32)
    inside = (position[:, None] >= begins[None, :]) & (position[:, None] < prompt_end[None, :])
    starts = jnp.sum(jnp.where(inside, begins[None, :], 0), axis=1)
    return (position, starts)


def attend(query_block, key_rot, value_rows, pos_block, start_block, position):
    scores = jnp.einsum(
        "qkrd,skd->krqs", query_block, key_rot, preferred_element_type=jnp.float32
    ) * (1.0 / math.sqrt(HD))
    allowed = (position[None, :] <= pos_block[:, None]) & (
        position[None, :] >= start_block[:, None]
    )
    masked = jnp.where(allowed[None, None], scores, -jnp.inf)
    row_max = jnp.max(masked, axis=-1, keepdims=True)
    exp_scores = jnp.exp(masked - row_max)
    probs = (exp_scores / jnp.sum(exp_scores, axis=-1, keepdims=True)).astype(jnp.bfloat16)
    return jnp.einsum(
        "krqs,skd->qkrd", probs, value_rows, preferred_element_type=jnp.float32
    ).astype(jnp.bfloat16)


def local_body(
    tokens,
    norm_gain,
    query_gain,
    key_gain,
    w_query,
    w_key,
    w_value,
    w_out,
    prompt_lengths,
    span_group,
):
    group_rows, width_local = tokens.shape
    groups = lax.axis_size(DP)
    arrival_rows = group_rows // groups
    device_index = lax.axis_index(DP)
    block_ids = jnp.arange(groups, dtype=jnp.int32)

    own_blocks = lax.dynamic_index_in_dim(span_group, device_index, 0, keepdims=False)
    same = own_blocks[:, None] == own_blocks[None, :]
    dup_rank = jnp.sum(same & (block_ids[None, :] < block_ids[:, None]), axis=1).astype(jnp.int32)
    first_dest = jnp.where(dup_rank == 0, own_blocks, groups)
    slot_source = jnp.zeros((groups,), jnp.int32).at[first_dest].set(block_ids, mode="drop")
    dup_block = jnp.sum(jnp.where(dup_rank == 1, block_ids, 0))
    token_blocks = tokens.reshape(groups, arrival_rows, width_local)
    dup_tokens = lax.dynamic_index_in_dim(token_blocks, dup_block, 0, keepdims=False)

    weights = jnp.concatenate([w_query, w_key, w_value, w_out], axis=1)
    weight_rows, weight_width = weights.shape
    packed = jnp.concatenate([weights, dup_tokens.reshape(weight_rows, -1)], axis=1)
    packed = lax.all_gather(packed, "y", axis=0, tiled=True)
    packed, token_blocks = lax.optimization_barrier((packed, token_blocks))
    packed = lax.all_gather(packed, "z", axis=0, tiled=True)
    weights = packed[:, :weight_width]
    dup_all = packed[:, weight_width:].reshape(groups, arrival_rows, width_local)

    outgoing = jnp.take(token_blocks, slot_source, axis=0, mode="clip")
    incoming = lax.all_to_all(outgoing, DP, split_axis=0, concat_axis=0, tiled=True)
    counts = jnp.sum((span_group == device_index).astype(jnp.int32), axis=1)
    offsets = jnp.cumsum(counts) - counts
    first_pos = jnp.where(counts >= 1, offsets, groups)
    second_pos = jnp.where(counts == 2, offsets + 1, groups)
    source_of = (
        jnp.zeros((groups,), jnp.int32)
        .at[first_pos]
        .set(block_ids, mode="drop")
        .at[second_pos]
        .set(block_ids + groups, mode="drop")
    )
    arrived = jnp.take(incoming, source_of, axis=0, mode="clip").reshape(group_rows, width_local)
    fsdp_size = lax.axis_size("fsdp")
    spread = jnp.broadcast_to(arrived[None], (fsdp_size,) + arrived.shape)
    pieces = lax.all_to_all(spread, "fsdp", split_axis=0, concat_axis=0, tiled=True)
    dup_source = jnp.sum(jnp.where(counts == 2, block_ids, 0))
    dup_target = jnp.sum(jnp.where(counts == 2, offsets + 1, 0))
    dup_mine = lax.dynamic_index_in_dim(dup_all, dup_source, 0, keepdims=False)
    dup_pieces = lax.all_gather(dup_mine, "fsdp", axis=0, tiled=False)
    pieces = lax.dynamic_update_slice_in_dim(pieces, dup_pieces, dup_target * arrival_rows, 1)
    cuts = [w_query.shape[1], w_key.shape[1], w_value.shape[1], w_out.shape[1]]
    bounds = [sum(cuts[:k]) for k in range(5)]
    query_full, key_full, value_full, out_full = (
        weights[:, bounds[k] : bounds[k + 1]] for k in range(4)
    )
    lengths = lax.dynamic_index_in_dim(prompt_lengths, device_index, 0, keepdims=False)
    position, starts = prompt_layout(lengths, group_rows)
    within = position - starts
    floats = pieces.astype(jnp.float32)
    normed = (
        floats
        * lax.rsqrt(jnp.mean(floats * floats, axis=(0, 2), keepdims=True) + epsilon)
        * norm_gain.astype(jnp.float32).reshape(fsdp_size, 1, width_local)
    ).astype(jnp.bfloat16)

    def project(matrix):
        return jnp.einsum(
            "fnk,fkc->nc",
            normed,
            matrix.reshape(fsdp_size, width_local, -1),
            preferred_element_type=jnp.float32,
        )

    query = project(query_full).reshape(group_rows, -1, HD)
    key_rows = project(key_full).reshape(group_rows, -1, HD)
    value_rows = project(value_full).reshape(group_rows, -1, HD).astype(jnp.bfloat16)
    query_rot = rotate(head_norm(query, query_gain), within).astype(jnp.bfloat16)
    key_rot = rotate(head_norm(key_rows, key_gain), within).astype(jnp.bfloat16)
    kv_heads = key_rot.shape[1]
    group_ratio = QH // KVH
    cache_rows = jnp.concatenate([key_rot, value_rows], axis=-1)
    block_count = group_rows // 512
    block_len = group_rows // block_count
    query_heads = query_rot.reshape(block_count, block_len, kv_heads, group_ratio, HD)

    def one_block(pieces):
        query_block, pos_block, start_block = pieces
        return attend(query_block, key_rot, value_rows, pos_block, start_block, position)

    mixed = lax.map(
        one_block,
        (
            query_heads,
            position.reshape(block_count, block_len),
            starts.reshape(block_count, block_len),
        ),
    )
    mixed = mixed.reshape(group_rows, kv_heads * group_ratio * HD)
    heads_all = lax.all_gather(mixed, "fsdp", axis=1, tiled=True)
    update = jnp.dot(heads_all, out_full, preferred_element_type=jnp.float32).astype(jnp.bfloat16)
    sub_ids = jnp.arange(2, dtype=jnp.int32)
    block_back = jnp.where(
        sub_ids[None, :] < counts[:, None], offsets[:, None] + sub_ids[None, :], 0
    ).reshape(-1)
    block_mine = own_blocks * 2 + dup_rank

    def send_back(rows):
        tail = rows.shape[1:]
        sent = jnp.take(
            rows.reshape((groups, arrival_rows) + tail), block_back, axis=0, mode="clip"
        ).reshape((groups, 2 * arrival_rows) + tail)
        back = lax.all_to_all(sent, DP, split_axis=0, concat_axis=0, tiled=True)
        return jnp.take(
            back.reshape((groups * 2, arrival_rows) + tail), block_mine, axis=0, mode="clip"
        ).reshape(rows.shape)

    cache_out = send_back(cache_rows)
    attention_out = send_back(update)
    return (attention_out, cache_out)


def solution(mesh):
    z_size = mesh.shape["dp"] // 4
    fine = Mesh(mesh.devices.reshape(z_size, 4, mesh.shape["fsdp"]), ("z", "y", "fsdp"))
    return jax.shard_map(
        local_body,
        mesh=fine,
        in_specs=(
            P(DP, "fsdp"),
            P(),
            P(),
            P(),
            P(DP, "fsdp"),
            P(DP, "fsdp"),
            P(DP, "fsdp"),
            P(DP, "fsdp"),
            P(),
            P(),
        ),
        out_specs=(P(DP, "fsdp"), P(DP, "fsdp", None)),
        check_vma=False,
    )
```

```python
import math

import jax
import jax.numpy as jnp
from jax import lax
from jax.sharding import Mesh, PartitionSpec as P

QH = 16
KVH = 8
HD = 128
DP = ("z", "y")


epsilon = 1e-06
rope_base = 1000000.0


def for_sending(x):

    def short(part):
        return part.astype(jnp.bfloat16) if part.dtype == jnp.float32 else part

    return jax.tree.map(short, x)


def head_norm(inputs, gains):
    inv_rms = lax.rsqrt(jnp.mean(inputs * inputs, axis=-1, keepdims=True) + epsilon)
    return inputs * inv_rms * gains.astype(jnp.float32)


def rotate(inputs, offsets):
    half_dim = inputs.shape[-1] // 2
    frequency = jnp.power(
        rope_base, -2.0 * jnp.arange(half_dim, dtype=jnp.float32) / inputs.shape[-1]
    )
    angles = offsets.astype(jnp.float32)[:, None] * frequency[None, :]
    cosine = jnp.cos(angles)[:, None, :]
    sine_part = jnp.sin(angles)[:, None, :]
    first_half = inputs[..., :half_dim]
    second = inputs[..., half_dim:]
    return jnp.concatenate(
        [first_half * cosine - second * sine_part, second * cosine + first_half * sine_part],
        axis=-1,
    )


def prompt_layout(lengths, group_rows):
    prompt_end = jnp.cumsum(lengths)
    begins = prompt_end - lengths
    position = jnp.arange(group_rows, dtype=jnp.int32)
    inside = (position[:, None] >= begins[None, :]) & (position[:, None] < prompt_end[None, :])
    starts = jnp.sum(jnp.where(inside, begins[None, :], 0), axis=1)
    return (position, starts)


def attend(query_block, key_rot, value_rows, pos_block, start_block, position):
    scores = jnp.einsum(
        "qkrd,skd->krqs", query_block, key_rot, preferred_element_type=jnp.float32
    ) * (1.0 / math.sqrt(HD))
    allowed = (position[None, :] <= pos_block[:, None]) & (
        position[None, :] >= start_block[:, None]
    )
    masked = jnp.where(allowed[None, None], scores, -jnp.inf)
    row_max = jnp.max(masked, axis=-1, keepdims=True)
    exp_scores = jnp.exp(masked - row_max)
    probs = (exp_scores / jnp.sum(exp_scores, axis=-1, keepdims=True)).astype(jnp.bfloat16)
    return jnp.einsum(
        "krqs,skd->qkrd", probs, value_rows, preferred_element_type=jnp.float32
    ).astype(jnp.bfloat16)


def local(
    tokens,
    norm_gain,
    query_gain,
    key_gain,
    w_query,
    w_key,
    w_value,
    w_out,
    prompt_lengths,
    span_group,
):
    group_rows, width_local = tokens.shape
    groups = lax.axis_size(DP)
    arrival_rows = group_rows // groups
    device_index = lax.axis_index(DP)
    block_ids = jnp.arange(groups, dtype=jnp.int32)

    own_blocks = lax.dynamic_index_in_dim(span_group, device_index, 0, keepdims=False)
    same = own_blocks[:, None] == own_blocks[None, :]
    dup_rank = jnp.sum(same & (block_ids[None, :] < block_ids[:, None]), axis=1).astype(jnp.int32)
    first_dest = jnp.where(dup_rank == 0, own_blocks, groups)
    slot_source = jnp.zeros((groups,), jnp.int32).at[first_dest].set(block_ids, mode="drop")
    dup_block = jnp.sum(jnp.where(dup_rank == 1, block_ids, 0))
    token_blocks = tokens.reshape(groups, arrival_rows, width_local)
    dup_tokens = lax.dynamic_index_in_dim(token_blocks, dup_block, 0, keepdims=False)

    weights = jnp.concatenate([w_query, w_key, w_value, w_out], axis=1)
    weight_rows, weight_width = weights.shape
    packed = jnp.concatenate([weights, dup_tokens.reshape(weight_rows, -1)], axis=1)
    packed = lax.all_gather(packed, "y", axis=0, tiled=True)
    packed, token_blocks = lax.optimization_barrier((packed, token_blocks))
    packed = lax.all_gather(packed, "z", axis=0, tiled=True)
    weights = packed[:, :weight_width]
    dup_all = packed[:, weight_width:].reshape(groups, arrival_rows, width_local)

    outgoing = jnp.take(token_blocks, slot_source, axis=0, mode="clip")
    incoming = lax.all_to_all(outgoing, DP, split_axis=0, concat_axis=0, tiled=True)
    counts = jnp.sum((span_group == device_index).astype(jnp.int32), axis=1)
    offsets = jnp.cumsum(counts) - counts
    first_pos = jnp.where(counts >= 1, offsets, groups)
    second_pos = jnp.where(counts == 2, offsets + 1, groups)
    source_of = (
        jnp.zeros((groups,), jnp.int32)
        .at[first_pos]
        .set(block_ids, mode="drop")
        .at[second_pos]
        .set(block_ids + groups, mode="drop")
    )
    arrived = jnp.take(incoming, source_of, axis=0, mode="clip").reshape(group_rows, width_local)
    fsdp_size = lax.axis_size("fsdp")
    spread = jnp.broadcast_to(arrived[None], (fsdp_size,) + arrived.shape)
    pieces = lax.all_to_all(spread, "fsdp", split_axis=0, concat_axis=0, tiled=True)
    dup_source = jnp.sum(jnp.where(counts == 2, block_ids, 0))
    dup_target = jnp.sum(jnp.where(counts == 2, offsets + 1, 0))
    dup_mine = lax.dynamic_index_in_dim(dup_all, dup_source, 0, keepdims=False)
    dup_pieces = lax.all_gather(dup_mine, "fsdp", axis=1, tiled=True)
    dup_pieces = dup_pieces.reshape(arrival_rows, fsdp_size, width_local).transpose(1, 0, 2)
    pieces = lax.dynamic_update_slice_in_dim(pieces, dup_pieces, dup_target * arrival_rows, 1)
    cuts = [w_query.shape[1], w_key.shape[1], w_value.shape[1], w_out.shape[1]]
    bounds = [sum(cuts[:k]) for k in range(5)]
    query_full, key_full, value_full, out_full = (
        weights[:, bounds[k] : bounds[k + 1]] for k in range(4)
    )
    lengths = lax.dynamic_index_in_dim(prompt_lengths, device_index, 0, keepdims=False)
    position, starts = prompt_layout(lengths, group_rows)
    within = position - starts
    floats = pieces.astype(jnp.float32)
    normed = (
        floats
        * lax.rsqrt(jnp.mean(floats * floats, axis=(0, 2), keepdims=True) + epsilon)
        * norm_gain.astype(jnp.float32).reshape(fsdp_size, 1, width_local)
    ).astype(jnp.bfloat16)

    def project(matrix):
        return jnp.einsum(
            "fnk,fkc->nc",
            normed,
            matrix.reshape(fsdp_size, width_local, -1),
            preferred_element_type=jnp.float32,
        )

    query = project(query_full).reshape(group_rows, -1, HD)
    key_rows = project(key_full).reshape(group_rows, -1, HD)
    value_rows = project(value_full).reshape(group_rows, -1, HD).astype(jnp.bfloat16)
    query_rot = rotate(head_norm(query, query_gain), within).astype(jnp.bfloat16)
    key_rot = rotate(head_norm(key_rows, key_gain), within).astype(jnp.bfloat16)
    kv_heads = key_rot.shape[1]
    group_ratio = QH // KVH
    cache_rows = jnp.concatenate([key_rot, value_rows], axis=-1)
    block_count = group_rows // 512
    block_len = group_rows // block_count
    query_heads = query_rot.reshape(block_count, block_len, kv_heads, group_ratio, HD)

    def one_block(pieces):
        query_block, pos_block, start_block = pieces
        return attend(query_block, key_rot, value_rows, pos_block, start_block, position)

    mixed = lax.map(
        one_block,
        (
            query_heads,
            position.reshape(block_count, block_len),
            starts.reshape(block_count, block_len),
        ),
    )
    mixed = mixed.reshape(group_rows, kv_heads * group_ratio * HD)
    heads_all = lax.all_gather(mixed, "fsdp", axis=1, tiled=True)
    update = jnp.dot(heads_all, out_full, preferred_element_type=jnp.float32).astype(jnp.bfloat16)
    sub_ids = jnp.arange(2, dtype=jnp.int32)
    block_back = jnp.where(
        sub_ids[None, :] < counts[:, None], offsets[:, None] + sub_ids[None, :], 0
    ).reshape(-1)
    block_mine = own_blocks * 2 + dup_rank

    def send_back(rows):
        tail = rows.shape[1:]
        sent = jnp.take(
            rows.reshape((groups, arrival_rows) + tail), block_back, axis=0, mode="clip"
        ).reshape((groups, 2 * arrival_rows) + tail)
        back = lax.all_to_all(sent, DP, split_axis=0, concat_axis=0, tiled=True)
        return jnp.take(
            back.reshape((groups * 2, arrival_rows) + tail), block_mine, axis=0, mode="clip"
        ).reshape(rows.shape)
    cache_out = send_back(cache_rows)
    attention_out = send_back(update)
    return (attention_out, cache_out)


def solution(mesh):
    z_size = mesh.shape["dp"] // 4
    fine = Mesh(mesh.devices.reshape(z_size, 4, mesh.shape["fsdp"]), ("z", "y", "fsdp"))
    return jax.shard_map(
        local,
        mesh=fine,
        in_specs=(
            P(DP, "fsdp"),
            P(),
            P(),
            P(),
            P(DP, "fsdp"),
            P(DP, "fsdp"),
            P(DP, "fsdp"),
            P(DP, "fsdp"),
            P(),
            P(),
        ),
        out_specs=(P(DP, "fsdp"), P(DP, "fsdp", None)),
        check_vma=False,
    )
```
